32 devices in a mesh: section: 4 (over y, x), mp: 2 (over core), dp: 4 (over z).
Axes of the slice: x: 2, y: 2, z: 4, core: 2. Of those that a mesh axis runs over, the one named last changes fastest.
Arguments:
- target_hidden: bfloat16 [4, 256, 8192], P('dp', None, 'section'), may hold values from -43 to 43, as said below
- embeds: bfloat16 [4, 256, 8192], P('dp', None, 'section'), may hold values from -50 to 50, as said below
- token_ids: int32 [4, 256], replicated, may hold values from 0 to 8191
- lengths: int32 [4], replicated, may hold values from 1 to 32, as said below
- offsets: int32 [4], replicated, may hold values from 0 to 224, as said below
- target_gain: float32 [8192], P('section'), may hold values from 0.5 to 1.5
- draft_gain: float32 [8192], P('section'), may hold values from 0.5 to 1.5
- head: bfloat16 [8192, 8192], P(('mp', 'dp'), 'section'), may hold values from -0.1875 to 0.1875
- fc_embed: bfloat16 [8192, 8192], P('section', ('mp', 'dp')), may hold values from -0.046875 to 0.046875
- fc_feature: bfloat16 [8192, 8192], P('section', ('mp', 'dp')), may hold values from -0.046875 to 0.046875
Outputs:
- loss: float32 [], replicated
- grad_embed: float32 [8192, 8192], P('section', ('mp', 'dp'))
- grad_feature: float32 [8192, 8192], P('section', ('mp', 'dp'))
The draws below stay inside these ranges and needn't reach their ends.
Inputs may be any that keep to these rules, and one draw needn't show every extreme that they name: `lengths`: they sum to 64, and the longest response has exactly 32 rows. offsets + lengths <= 256 in every sequence; the sequence of the longest response starts at 224. `target_hidden`: real-valued features. `embeds`: real-valued embeddings.
All inputs are finite; a program needn't handle non-finite values.
Results may differ from the reference program's by a relative error of at most 0.0035.
The reference program's roundings to bfloat16 on the way (of `features`, `target_norm`, `draft_norm`, `logit_grad` and `hidden_grad`) count: a program that leaves them out, or rounds other values in their place, can miss the bound.
Values may be sent and summed in bfloat16 or wider, within the bound.
No kernel may reach another device: no remote copies, remote signals or barrier semaphores. Data moves between devices by JAX's collectives and lax.ppermute only.
A program may use at most 64 MiB of HBM per device.

```python
import math
import jax
import jax.numpy as jnp
import numpy as np
from jax import lax

D = 8192
LEN = 256
VOCAB = 8192
SEQS = 4
R_TOT = 64
MOST = 32


def response_plan(key):
    base = jax.random.fold_in(key, 17)
    key_weight, key_place, key_offset = jax.random.split(base, 3)
    rest_rows = R_TOT - MOST
    weights = jax.random.randint(key_weight, (SEQS - 1,), 4, 8)
    shares = rest_rows * weights // jnp.sum(weights)
    missing = rest_rows - jnp.sum(shares)
    shares = shares + (jnp.arange(SEQS - 1) < missing).astype(jnp.int32)
    longest = jax.random.randint(key_place, (), 0, SEQS)
    index_all = jnp.arange(SEQS)
    lower_pick = jnp.clip(index_all, 0, SEQS - 2)
    upper_pick = jnp.clip(index_all - 1, 0, SEQS - 2)
    lengths = jnp.where(index_all < longest, shares[lower_pick], jnp.where(index_all == longest, MOST, shares[upper_pick]))
    lengths = lengths.astype(jnp.int32)
    offsets = jax.random.randint(key_offset, (SEQS,), 0, LEN - MOST + 1)
    offsets = jnp.where(index_all == longest, LEN - MOST, offsets)
    return (lengths, offsets.astype(jnp.int32))


def draw_lengths(key, part):
    return response_plan(key)[0]


def draw_offsets(key, part):
    return response_plan(key)[1]


def rough_rows(key, shape, shared):
    key_base, key_row, key_col, key_common = jax.random.split(key, 4)
    values = jnp.clip(jax.random.normal(key_base, shape, jnp.float32), -6.0, 6.0)
    row_scale = jnp.exp(jax.random.uniform(key_row, shape[:-1] + (1,), jnp.float32, -1.15, 1.15))
    col_scale = jnp.exp(jax.random.uniform(key_col, (shape[-1],), jnp.float32, -0.8, 0.8))
    common = jnp.clip(1.2 * jax.random.normal(key_common, (shape[-1],), jnp.float32), -3.6, 3.6)
    return (values * row_scale + shared * common) * col_scale


def draw_target_hidden(key, part):
    return rough_rows(jax.random.fold_in(key, 3), (SEQS, LEN, D), 0.0).astype(jnp.bfloat16)


def draw_embeds(key, part):
    return rough_rows(jax.random.fold_in(key, 5), (SEQS, LEN, D), 1.0).astype(jnp.bfloat16)


def plant(values, stream_key, low, largest):
    shape = values.shape
    spot = [jax.random.randint(jax.random.fold_in(stream_key, axis), (), 0, shape[axis]) for axis in range(len(shape))]
    values = values.at[tuple(spot)].set(low)
    longest = shape.index(max(shape))
    spot[longest] = (spot[longest] + 1) % shape[longest]
    return values.at[tuple(spot)].set(largest)


def block_levels(own_key, dims, cuts, least, top_value):
    level = 1.0
    for dim, parts in cuts:
        heights = jax.random.uniform(jax.random.fold_in(jax.random.fold_in(own_key, 6), dim), (parts,), jnp.float32, least / len(cuts), top_value / len(cuts))
        level = level * jnp.repeat(jnp.exp(heights), dims[dim] // parts).reshape((-1,) + (1,) * (len(dims) - 1 - dim))
    return level


def cumulative_ranks(count, slope):
    loads = [(1 << 20) // math.isqrt(standing ** slope) + 1 for standing in range(1, count + 1)]
    deviation = 1 + sum(loads) // (1 << 30)
    return np.cumsum(np.array([max(1, weight // deviation) for weight in loads]))


def skewed_ids(key, extent, amount, skew):
    table = cumulative_ranks(amount, skew)
    pick = jax.random.randint(jax.random.fold_in(key, 1), extent, 0, int(table[amount - 1]))
    standing = jnp.searchsorted(jnp.asarray(table, jnp.int32), pick, side="right")
    return jax.random.permutation(jax.random.fold_in(key, 2), amount)[standing].astype(jnp.int32)


def bell_draw(stream_key, shape, width, most, pieces=(), held_as=jnp.bfloat16):
    loudness = block_levels(stream_key, shape, pieces, -0.22, 0.18) if pieces else 1.0
    result = jax.random.normal(stream_key, shape, jnp.float32) * width * loudness
    return jnp.minimum(jnp.maximum(result, -most), most).astype(held_as)


def setup_inputs(seed: int = 0) -> dict:
    streams_of = jax.random.split(jax.random.key(seed), 11)
    return {
        "target_hidden": draw_target_hidden(jax.random.fold_in(streams_of[10], 71), 0),
        "embeds": draw_embeds(jax.random.fold_in(streams_of[10], 71), 0),
        "token_ids": plant(skewed_ids(streams_of[2], (SEQS, LEN), VOCAB, 2), jax.random.fold_in(streams_of[2], 3), 0, VOCAB - 1).astype(jnp.int32),
        "lengths": draw_lengths(jax.random.fold_in(streams_of[10], 71), 0),
        "offsets": draw_offsets(jax.random.fold_in(streams_of[10], 71), 0),
        "target_gain": jnp.clip(1.0 + 0.1 * jax.random.normal(streams_of[5], (D,), jnp.float32), 0.5, 1.5),
        "draft_gain": jnp.clip(1.0 + 0.1 * jax.random.normal(streams_of[6], (D,), jnp.float32), 0.5, 1.5),
        "head": bell_draw(streams_of[7], (VOCAB, D), (D // 9) ** -0.5, 0.1875, ((0, 8), (1, 4))),
        "fc_embed": bell_draw(streams_of[8], (D, D), (2 * D) ** -0.5, 0.046875, ((0, 4), (1, 8))),
        "fc_feature": bell_draw(streams_of[9], (D, D), (2 * D) ** -0.5, 0.046875, ((0, 4), (1, 8))),
    }


z_weight = 0.004
label_mix = 0.1
eps_norm = 1e-05

def contract_last(operand, weights):
    return lax.dot_general(operand, weights, (((1,), (1,)), ((), ())), preferred_element_type=jnp.float32)

def contract_first(operand, weights):
    return lax.dot_general(operand, weights, (((0,), (0,)), ((), ())), preferred_element_type=jnp.float32)

def reference(target_hidden, embeds, token_ids, lengths, offsets, target_gain, draft_gain, head, fc_embed, fc_feature):
    starts = (jnp.cumsum(lengths) - lengths).astype(jnp.int32)
    packed = jnp.arange(R_TOT, dtype=jnp.int32)
    source = (lax.optimization_barrier(jnp.sum((starts[None, :] <= packed[:, None]).astype(jnp.int32), axis=1)) - 1).astype(jnp.int32)
    position = (offsets[source] + packed - starts[source]).astype(jnp.int32)
    features = target_hidden[source, position]
    embedding = embeds[source, position]
    labels = token_ids[source, position]
    target_scale = lax.rsqrt(lax.optimization_barrier(jnp.sum(jnp.square(features.astype(jnp.float32)), axis=1)) / D + eps_norm)
    target_norm = (features.astype(jnp.float32) * target_scale[:, None] * target_gain).astype(jnp.bfloat16)
    hidden = jnp.dot(embedding, fc_embed, preferred_element_type=jnp.float32) + jnp.dot(features, fc_feature, preferred_element_type=jnp.float32)
    draft_scale = lax.rsqrt(lax.optimization_barrier(jnp.sum(hidden * hidden, axis=1)) / D + eps_norm)
    draft_norm = (hidden * draft_scale[:, None] * draft_gain).astype(jnp.bfloat16)
    target_logit = contract_last(target_norm, head)
    draft_logit = contract_last(draft_norm, head)
    is_label = labels[:, None] == jnp.arange(VOCAB, dtype=jnp.int32)[None, :]
    target_exp = jnp.exp(target_logit)
    target_total = lax.optimization_barrier(jnp.sum(target_exp, axis=1))
    cross_total = lax.optimization_barrier(jnp.sum(target_exp * draft_logit, axis=1))
    draft_total = lax.optimization_barrier(jnp.sum(jnp.exp(draft_logit), axis=1))
    label_logit = lax.optimization_barrier(jnp.sum(jnp.where(is_label, draft_logit, 0.0), axis=1))
    draft_lse = jnp.log(draft_total)
    target_lse = jnp.log(target_total)
    row_loss = draft_lse - (1.0 - label_mix) * cross_total / target_total - label_mix * label_logit + z_weight * draft_lse * draft_lse
    loss = jnp.mean(row_loss)
    logit_grad = ((1.0 + 2.0 * z_weight * draft_lse)[:, None] * jnp.exp(draft_logit - draft_lse[:, None]) - (1.0 - label_mix) * jnp.exp(target_logit - target_lse[:, None]) - label_mix * is_label.astype(jnp.float32)).astype(jnp.bfloat16)
    draft_grad = jnp.dot(logit_grad, head, preferred_element_type=jnp.float32)
    upstream = draft_grad * draft_gain
    inner_sum = lax.optimization_barrier(jnp.sum(hidden * upstream, axis=1))
    hidden_grad = (draft_scale[:, None] * upstream - hidden * (draft_scale ** 3 * inner_sum / D)[:, None]).astype(jnp.bfloat16)
    grad_embed = contract_first(embedding, hidden_grad)
    grad_feature = contract_first(features, hidden_grad)
    return (loss, grad_embed, grad_feature)
```

```python
import jax
import jax.numpy as jnp
from jax import lax
from jax.sharding import PartitionSpec as P

D = 8192
R_OWN = 8


z_weight = 0.004
label_mix = 0.1
eps_norm = 1e-05

ALL = ("section", "mp", "dp")


def contract_last(operand, weights):
    return lax.dot_general(
        operand, weights, (((1,), (1,)), ((), ())), preferred_element_type=jnp.float32
    )


def contract_first(operand, weights):
    return lax.dot_general(
        operand, weights, (((0,), (0,)), ((), ())), preferred_element_type=jnp.float32
    )


def sequence_of(packed, starts):
    return jnp.sum((starts[None, :] <= packed[:, None]).astype(jnp.int32), axis=1) - 1


def exchange(send, axes):
    return lax.all_to_all(send, axes, split_axis=0, concat_axis=0, tiled=True)


def gather_axis(x, axis):
    count = lax.axis_size(axis)
    if count == 2:
        other = lax.ppermute(x, axis, [(0, 1), (1, 0)])
        mine = lax.axis_index(axis)
        return jnp.where(mine == 0, jnp.stack([x, other]), jnp.stack([other, x]))
    return exchange(jnp.broadcast_to(x[None], (count,) + x.shape), axis)


def pad_cols(count):
    return -(-count // 128) * 128


def on_device(
    target_hidden,
    embeds,
    token_ids,
    lengths,
    offsets,
    target_gain,
    draft_gain,
    head,
    fc_embed,
    fc_feature,
):
    count_dp = lax.axis_size("dp")
    count_mp = lax.axis_size("mp")
    count_sec = lax.axis_size("section")
    groups = count_mp * count_dp
    n_dev = count_sec * groups
    my_dp = lax.axis_index("dp")
    my_mp = lax.axis_index("mp")
    my_sec = lax.axis_index("section")
    me = (my_sec * count_mp + my_mp) * count_dp + my_dp
    width = target_hidden.shape[2]
    seq_len = target_hidden.shape[1]
    vocab_tile = head.shape[0]
    block = fc_embed.shape[1]
    full_width = width * count_sec
    total_rows = R_OWN * groups
    per_dev = total_rows // n_dev
    half = 2 * R_OWN
    starts = jnp.cumsum(lengths) - lengths

    gain_full = gather_axis(draft_gain, "section").reshape(full_width)

    slot = my_mp * half + jnp.arange(half, dtype=jnp.int32)
    pos = jnp.clip(offsets[my_dp] + slot, 0, seq_len - 1)
    mine = jnp.stack([jnp.take(embeds[0], pos, axis=0), jnp.take(target_hidden[0], pos, axis=0)])
    by_dp = exchange(jnp.broadcast_to(mine[None], (count_dp,) + mine.shape), "dp")
    every = gather_axis(by_dp, "mp")
    every = every.transpose(2, 0, 1, 3, 4).reshape(2, count_mp * count_dp * half, width)
    packed = jnp.arange(total_rows, dtype=jnp.int32)
    seq_all = sequence_of(packed, starts)
    slot_all = packed - starts[seq_all]
    pick = ((slot_all // half) * count_dp + seq_all) * half + slot_all % half
    embed_all = jnp.take(every[0], pick, axis=0)
    feature_all = jnp.take(every[1], pick, axis=0)
    position_all = offsets[seq_all] + slot_all
    labels_all = token_ids.reshape(-1)[seq_all * seq_len + position_all]
    my_rows = me * per_dev + jnp.arange(per_dev, dtype=jnp.int32)
    labels = labels_all[my_rows]

    partial_value = jnp.dot(embed_all, fc_embed, preferred_element_type=jnp.float32) + jnp.dot(
        feature_all, fc_feature, preferred_element_type=jnp.float32
    )
    target_square = jnp.sum(jnp.square(feature_all.astype(jnp.float32)), axis=1)
    spare = total_rows // per_dev
    extra = jnp.pad(target_square.reshape(per_dev, spare), ((0, 0), (0, pad_cols(spare) - spare)))
    send1 = jnp.concatenate(
        [
            partial_value.reshape(n_dev, per_dev, block),
            jnp.broadcast_to(extra[None], (n_dev,) + extra.shape),
        ],
        axis=2,
    )
    got1 = exchange(send1, ALL).reshape(count_sec, groups, per_dev, -1)
    hidden = (
        jnp.sum(got1[..., :block], axis=0).transpose(1, 0, 2).reshape(per_dev, groups * block)
    )
    target_square = jnp.sum(got1[:, 0, :, block : block + spare], axis=0).reshape(total_rows)
    target_scale = lax.rsqrt(target_square / D + eps_norm)
    target_norm = (feature_all.astype(jnp.float32) * target_scale[:, None] * target_gain).astype(
        jnp.bfloat16
    )
    draft_square = jnp.sum(hidden * hidden, axis=1)
    draft_scale = lax.rsqrt(draft_square / D + eps_norm)
    draft_norm = (hidden * draft_scale[:, None] * gain_full).astype(jnp.bfloat16)

    send2 = jnp.broadcast_to(
        draft_norm.reshape(per_dev, count_sec, 1, width).transpose(1, 2, 0, 3),
        (count_sec, groups, per_dev, width),
    ).reshape(n_dev, per_dev, width)
    draft_norm_all = exchange(send2, ALL).reshape(total_rows, width)

    target_part = contract_last(target_norm, head)
    draft_part = contract_last(draft_norm_all, head)
    send3 = (
        jnp.stack([target_part, draft_part])
        .reshape(2, n_dev, per_dev, vocab_tile)
        .transpose(1, 0, 2, 3)
    )
    got3 = exchange(send3, ALL).reshape(count_sec, groups, 2, per_dev, vocab_tile)
    logits = jnp.sum(got3, axis=0).transpose(1, 2, 0, 3).reshape(2, per_dev, groups * vocab_tile)
    target_logit, draft_logit = logits[0], logits[1]
    vocab = groups * vocab_tile
    is_label = labels[:, None] == jnp.arange(vocab, dtype=jnp.int32)[None, :]
    target_exp = jnp.exp(target_logit)
    target_total = jnp.sum(target_exp, axis=1)
    cross_total = jnp.sum(target_exp * draft_logit, axis=1)
    draft_total = jnp.sum(jnp.exp(draft_logit), axis=1)
    label_logit = jnp.sum(jnp.where(is_label, draft_logit, 0.0), axis=1)
    draft_lse = jnp.log(draft_total)
    target_lse = jnp.log(target_total)
    row_loss = (
        draft_lse
        - (1.0 - label_mix) * cross_total / target_total
        - label_mix * label_logit
        + z_weight * draft_lse * draft_lse
    )
    logit_grad = (
        (
            (1.0 + 2.0 * z_weight * draft_lse)[:, None] * jnp.exp(draft_logit - draft_lse[:, None])
            - (1.0 - label_mix) * jnp.exp(target_logit - target_lse[:, None])
            - label_mix * is_label.astype(jnp.float32)
        )
    ).astype(jnp.bfloat16)

    send4 = jnp.broadcast_to(
        logit_grad.reshape(per_dev, 1, groups, vocab_tile).transpose(1, 2, 0, 3),
        (count_sec, groups, per_dev, vocab_tile),
    ).reshape(n_dev, per_dev, vocab_tile)
    grad_tile = exchange(send4, ALL).reshape(total_rows, vocab_tile)

    grad_part = jnp.dot(grad_tile, head, preferred_element_type=jnp.float32)
    loss_cols = jnp.pad(row_loss[:, None], ((0, 0), (0, 127)))
    send5 = jnp.concatenate(
        [
            grad_part.reshape(n_dev, per_dev, width),
            jnp.broadcast_to(loss_cols[None], (n_dev,) + loss_cols.shape),
        ],
        axis=2,
    )
    got5 = exchange(send5, ALL).reshape(count_sec, groups, per_dev, -1)
    draft_grad = (
        jnp.sum(got5[..., :width], axis=1).transpose(1, 0, 2).reshape(per_dev, full_width)
    )
    loss = jnp.mean(got5[..., width].reshape(total_rows))
    upstream = draft_grad * gain_full
    inner_sum = jnp.sum(hidden * upstream, axis=1)
    hidden_grad = (
        draft_scale[:, None] * upstream - hidden * (draft_scale**3 * inner_sum / D)[:, None]
    ).astype(jnp.bfloat16)

    send6 = jnp.broadcast_to(
        hidden_grad.reshape(per_dev, 1, groups, block).transpose(1, 2, 0, 3),
        (count_sec, groups, per_dev, block),
    ).reshape(n_dev, per_dev, block)
    block_grad = exchange(send6, ALL).reshape(total_rows, block)
    grad_embed = contract_first(embed_all, block_grad)
    grad_feature = contract_first(feature_all, block_grad)
    return (loss, grad_embed, grad_feature)


def solution(mesh):
    return jax.shard_map(
        on_device,
        mesh=mesh,
        in_specs=(
            P("dp", None, "section"),
            P("dp", None, "section"),
            P(),
            P(),
            P(),
            P("section"),
            P("section"),
            P(("mp", "dp"), "section"),
            P("section", ("mp", "dp")),
            P("section", ("mp", "dp")),
        ),
        out_specs=(P(), P("section", ("mp", "dp")), P("section", ("mp", "dp"))),
        check_vma=False,
    )
```

```python
import jax
import jax.numpy as jnp
from jax import lax
from jax.sharding import PartitionSpec as P

D = 8192
R_OWN = 8


z_weight = 0.004
label_mix = 0.1
eps_norm = 1e-05

ALL = ("section", "mp", "dp")


def contract_last(operand, weights):
    return lax.dot_general(
        operand, weights, (((1,), (1,)), ((), ())), preferred_element_type=jnp.float32
    )


def contract_first(operand, weights):
    return lax.dot_general(
        operand, weights, (((0,), (0,)), ((), ())), preferred_element_type=jnp.float32
    )


def sequence_of(packed, starts):
    return jnp.sum((starts[None, :] <= packed[:, None]).astype(jnp.int32), axis=1) - 1


def exchange(send, axes):
    return lax.all_to_all(send, axes, split_axis=0, concat_axis=0, tiled=True)


def shifted(x, axis):
    count = lax.axis_size(axis)
    parts = [x] + [
        lax.ppermute(x, axis, [(i, (i + k) % count) for i in range(count)])
        for k in range(1, count)
    ]
    return jnp.stack(parts)


def pad_cols(count):
    return -(-count // 128) * 128


def on_device(
    target_hidden,
    embeds,
    token_ids,
    lengths,
    offsets,
    target_gain,
    draft_gain,
    head,
    fc_embed,
    fc_feature,
):
    count_dp = lax.axis_size("dp")
    count_mp = lax.axis_size("mp")
    count_sec = lax.axis_size("section")
    groups = count_mp * count_dp
    n_dev = count_sec * groups
    my_dp = lax.axis_index("dp")
    my_mp = lax.axis_index("mp")
    my_sec = lax.axis_index("section")
    me = (my_sec * count_mp + my_mp) * count_dp + my_dp
    width = target_hidden.shape[2]
    seq_len = target_hidden.shape[1]
    vocab_tile = head.shape[0]
    block = fc_embed.shape[1]
    full_width = width * count_sec
    total_rows = R_OWN * groups
    per_dev = total_rows // n_dev
    half = 2 * R_OWN
    starts = jnp.cumsum(lengths) - lengths

    by_shift = shifted(draft_gain, "section")
    gain_full = jnp.take(
        by_shift, (my_sec - jnp.arange(count_sec, dtype=jnp.int32)) % count_sec, axis=0
    ).reshape(full_width)

    slot = my_mp * half + jnp.arange(half, dtype=jnp.int32)
    pos = jnp.clip(offsets[my_dp] + slot, 0, seq_len - 1)
    mine = jnp.stack([jnp.take(embeds[0], pos, axis=0), jnp.take(target_hidden[0], pos, axis=0)])
    every = shifted(shifted(mine, "dp"), "mp")
    every = every.transpose(2, 0, 1, 3, 4).reshape(2, count_mp * count_dp * half, width)
    packed = jnp.arange(total_rows, dtype=jnp.int32)
    seq_all = sequence_of(packed, starts)
    slot_all = packed - starts[seq_all]
    shift_mp = (my_mp - slot_all // half) % count_mp
    shift_dp = (my_dp - seq_all) % count_dp
    pick = (shift_mp * count_dp + shift_dp) * half + slot_all % half
    embed_all = jnp.take(every[0], pick, axis=0)
    feature_all = jnp.take(every[1], pick, axis=0)
    position_all = offsets[seq_all] + slot_all
    labels_all = token_ids.reshape(-1)[seq_all * seq_len + position_all]
    my_rows = me * per_dev + jnp.arange(per_dev, dtype=jnp.int32)
    labels = labels_all[my_rows]

    partial_value = jnp.dot(embed_all, fc_embed, preferred_element_type=jnp.float32) + jnp.dot(
        feature_all, fc_feature, preferred_element_type=jnp.float32
    )
    target_square = jnp.sum(jnp.square(feature_all.astype(jnp.float32)), axis=1)
    spare = total_rows // per_dev
    extra = jnp.pad(target_square.reshape(per_dev, spare), ((0, 0), (0, pad_cols(spare) - spare)))
    send1 = jnp.concatenate(
        [
            partial_value.reshape(n_dev, per_dev, block),
            jnp.broadcast_to(extra[None], (n_dev,) + extra.shape),
        ],
        axis=2,
    )
    got1 = exchange(send1, ALL).reshape(count_sec, groups, per_dev, -1)
    hidden = (
        jnp.sum(got1[..., :block], axis=0).transpose(1, 0, 2).reshape(per_dev, groups * block)
    )
    target_square = jnp.sum(got1[:, 0, :, block : block + spare], axis=0).reshape(total_rows)
    target_scale = lax.rsqrt(target_square / D + eps_norm)
    target_norm = (feature_all.astype(jnp.float32) * target_scale[:, None] * target_gain).astype(
        jnp.bfloat16
    )
    draft_square = jnp.sum(hidden * hidden, axis=1)
    draft_scale = lax.rsqrt(draft_square / D + eps_norm)
    draft_norm = (hidden * draft_scale[:, None] * gain_full).astype(jnp.bfloat16)

    send2 = jnp.broadcast_to(
        draft_norm.reshape(per_dev, count_sec, 1, width).transpose(1, 2, 0, 3),
        (count_sec, groups, per_dev, width),
    ).reshape(n_dev, per_dev, width)
    draft_norm_all = exchange(send2, ALL).reshape(total_rows, width)

    target_part = contract_last(target_norm, head)
    draft_part = contract_last(draft_norm_all, head)
    send3 = (
        jnp.stack([target_part, draft_part])
        .reshape(2, n_dev, per_dev, vocab_tile)
        .transpose(1, 0, 2, 3)
    )
    got3 = exchange(send3, ALL).reshape(count_sec, groups, 2, per_dev, vocab_tile)
    logits = jnp.sum(got3, axis=0).transpose(1, 2, 0, 3).reshape(2, per_dev, groups * vocab_tile)
    target_logit, draft_logit = logits[0], logits[1]
    vocab = groups * vocab_tile
    is_label = labels[:, None] == jnp.arange(vocab, dtype=jnp.int32)[None, :]
    target_exp = jnp.exp(target_logit)
    target_total = jnp.sum(target_exp, axis=1)
    cross_total = jnp.sum(target_exp * draft_logit, axis=1)
    draft_total = jnp.sum(jnp.exp(draft_logit), axis=1)
    label_logit = jnp.sum(jnp.where(is_label, draft_logit, 0.0), axis=1)
    draft_lse = jnp.log(draft_total)
    target_lse = jnp.log(target_total)
    row_loss = (
        draft_lse
        - (1.0 - label_mix) * cross_total / target_total
        - label_mix * label_logit
        + z_weight * draft_lse * draft_lse
    )
    logit_grad = (
        (
            (1.0 + 2.0 * z_weight * draft_lse)[:, None] * jnp.exp(draft_logit - draft_lse[:, None])
            - (1.0 - label_mix) * jnp.exp(target_logit - target_lse[:, None])
            - label_mix * is_label.astype(jnp.float32)
        )
    ).astype(jnp.bfloat16)

    send4 = jnp.broadcast_to(
        logit_grad.reshape(per_dev, 1, groups, vocab_tile).transpose(1, 2, 0, 3),
        (count_sec, groups, per_dev, vocab_tile),
    ).reshape(n_dev, per_dev, vocab_tile)
    grad_tile = exchange(send4, ALL).reshape(total_rows, vocab_tile)

    grad_part = jnp.dot(grad_tile, head, preferred_element_type=jnp.float32)
    loss_cols = jnp.pad(row_loss[:, None], ((0, 0), (0, 127)))
    send5 = jnp.concatenate(
        [
            grad_part.reshape(n_dev, per_dev, width),
            jnp.broadcast_to(loss_cols[None], (n_dev,) + loss_cols.shape),
        ],
        axis=2,
    )
    got5 = exchange(send5, ALL).reshape(count_sec, groups, per_dev, -1)
    draft_grad = (
        jnp.sum(got5[..., :width], axis=1).transpose(1, 0, 2).reshape(per_dev, full_width)
    )
    loss = jnp.mean(got5[..., width].reshape(total_rows))
    upstream = draft_grad * gain_full
    inner_sum = jnp.sum(hidden * upstream, axis=1)
    hidden_grad = (
        draft_scale[:, None] * upstream - hidden * (draft_scale**3 * inner_sum / D)[:, None]
    ).astype(jnp.bfloat16)

    send6 = jnp.broadcast_to(
        hidden_grad.reshape(per_dev, 1, groups, block).transpose(1, 2, 0, 3),
        (count_sec, groups, per_dev, block),
    ).reshape(n_dev, per_dev, block)
    block_grad = exchange(send6, ALL).reshape(total_rows, block)
    grad_embed = contract_first(embed_all, block_grad)
    grad_feature = contract_first(feature_all, block_grad)
    return (loss, grad_embed, grad_feature)


def solution(mesh):
    return jax.shard_map(
        on_device,
        mesh=mesh,
        in_specs=(
            P("dp", None, "section"),
            P("dp", None, "section"),
            P(),
            P(),
            P(),
            P("section"),
            P("section"),
            P(("mp", "dp"), "section"),
            P("section", ("mp", "dp")),
            P("section", ("mp", "dp")),
        ),
        out_specs=(P(), P("section", ("mp", "dp")), P("section", ("mp", "dp"))),
        check_vma=False,
    )
```

```python
import jax
import jax.numpy as jnp
from jax import lax
from jax.sharding import PartitionSpec as P

D = 8192
R_OWN = 8


z_weight = 0.004
label_mix = 0.1
eps_norm = 1e-05

ALL = ("section", "mp", "dp")


def contract_last(operand, weights):
    return lax.dot_general(
        operand, weights, (((1,), (1,)), ((), ())), preferred_element_type=jnp.float32
    )


def contract_first(operand, weights):
    return lax.dot_general(
        operand, weights, (((0,), (0,)), ((), ())), preferred_element_type=jnp.float32
    )


def sequence_of(packed, starts):
    return jnp.sum((starts[None, :] <= packed[:, None]).astype(jnp.int32), axis=1) - 1


def exchange(send, axes):
    return lax.all_to_all(send, axes, split_axis=0, concat_axis=0, tiled=True)


def shifted(x, axis):
    count = lax.axis_size(axis)
    parts = [x] + [
        lax.ppermute(x, axis, [(i, (i + k) % count) for i in range(count)])
        for k in range(1, count)
    ]
    return jnp.stack(parts)


def pad_cols(count):
    return -(-count // 128) * 128


def on_device(
    target_hidden,
    embeds,
    token_ids,
    lengths,
    offsets,
    target_gain,
    draft_gain,
    head,
    fc_embed,
    fc_feature,
):
    count_dp = lax.axis_size("dp")
    count_mp = lax.axis_size("mp")
    count_sec = lax.axis_size("section")
    groups = count_mp * count_dp
    n_dev = count_sec * groups
    my_dp = lax.axis_index("dp")
    my_mp = lax.axis_index("mp")
    my_sec = lax.axis_index("section")
    me = (my_sec * count_mp + my_mp) * count_dp + my_dp
    width = target_hidden.shape[2]
    seq_len = target_hidden.shape[1]
    vocab_tile = head.shape[0]
    block = fc_embed.shape[1]
    full_width = width * count_sec
    total_rows = R_OWN * groups
    per_dev = total_rows // n_dev
    half = 2 * R_OWN
    starts = jnp.cumsum(lengths) - lengths

    first = jnp.minimum(offsets[my_dp] + my_mp * half, seq_len - half)
    mine = jnp.stack(
        [
            lax.dynamic_slice_in_dim(embeds[0], first, half, axis=0),
            lax.dynamic_slice_in_dim(target_hidden[0], first, half, axis=0),
        ]
    )
    every = shifted(shifted(mine, "dp"), "mp")
    every = every.transpose(2, 0, 1, 3, 4).reshape(2, count_mp * count_dp * half, width)
    packed = jnp.arange(total_rows, dtype=jnp.int32)
    seq_all = sequence_of(packed, starts)
    slot_all = packed - starts[seq_all]
    shift_mp = (my_mp - slot_all // half) % count_mp
    shift_dp = (my_dp - seq_all) % count_dp
    base = offsets[seq_all] + (slot_all // half) * half
    lag = base - jnp.minimum(base, seq_len - half)
    within = jnp.minimum(slot_all % half + lag, half - 1)
    pick = (shift_mp * count_dp + shift_dp) * half + within
    embed_all = jnp.take(every[0], pick, axis=0)
    feature_all = jnp.take(every[1], pick, axis=0)
    position_all = offsets[seq_all] + slot_all
    labels_all = token_ids.reshape(-1)[seq_all * seq_len + position_all]
    my_rows = me * per_dev + jnp.arange(per_dev, dtype=jnp.int32)
    labels = labels_all[my_rows]

    partial_value = jnp.dot(embed_all, fc_embed, preferred_element_type=jnp.float32) + jnp.dot(
        feature_all, fc_feature, preferred_element_type=jnp.float32
    )
    target_square = jnp.sum(jnp.square(feature_all.astype(jnp.float32)), axis=1)
    piece = width // groups
    spare = pad_cols(-(-(total_rows + piece) // per_dev))
    gain_piece = lax.dynamic_slice_in_dim(draft_gain, (my_mp * count_dp + my_dp) * piece, piece)
    extra = jnp.pad(
        jnp.concatenate([target_square, gain_piece]),
        (0, per_dev * spare - total_rows - piece),
    ).reshape(per_dev, spare)
    send1 = jnp.concatenate(
        [
            partial_value.reshape(n_dev, per_dev, block),
            jnp.broadcast_to(extra[None], (n_dev,) + extra.shape),
        ],
        axis=2,
    )
    got1 = exchange(send1, ALL).reshape(count_sec, groups, per_dev, -1)
    hidden = (
        jnp.sum(got1[..., :block], axis=0).transpose(1, 0, 2).reshape(per_dev, groups * block)
    )
    extra_got = got1[..., block:].reshape(count_sec, groups, per_dev * spare)
    target_square = jnp.sum(extra_got[:, 0, :total_rows], axis=0)
    gain_full = extra_got[:, :, total_rows : total_rows + piece].reshape(full_width)
    target_scale = lax.rsqrt(target_square / D + eps_norm)
    target_norm = (feature_all.astype(jnp.float32) * target_scale[:, None] * target_gain).astype(
        jnp.bfloat16
    )
    draft_square = jnp.sum(hidden * hidden, axis=1)
    draft_scale = lax.rsqrt(draft_square / D + eps_norm)
    draft_norm = (hidden * draft_scale[:, None] * gain_full).astype(jnp.bfloat16)

    send2 = jnp.broadcast_to(
        draft_norm.reshape(per_dev, count_sec, 1, width).transpose(1, 2, 0, 3),
        (count_sec, groups, per_dev, width),
    ).reshape(n_dev, per_dev, width)
    draft_norm_all = exchange(send2, ALL).reshape(total_rows, width)

    target_part = contract_last(target_norm, head)
    draft_part = contract_last(draft_norm_all, head)
    send3 = jnp.stack([target_part, draft_part]).reshape(2, n_dev, per_dev, vocab_tile)
    got3 = lax.all_to_all(send3, ALL, split_axis=1, concat_axis=1, tiled=True)
    got3 = got3.reshape(2, count_sec, groups, per_dev, vocab_tile)
    logits = jnp.sum(got3, axis=1).transpose(0, 2, 1, 3).reshape(2, per_dev, groups * vocab_tile)
    target_logit, draft_logit = logits[0], logits[1]
    vocab = groups * vocab_tile
    is_label = labels[:, None] == jnp.arange(vocab, dtype=jnp.int32)[None, :]
    target_exp = jnp.exp(target_logit)
    target_total = jnp.sum(target_exp, axis=1)
    cross_total = jnp.sum(target_exp * draft_logit, axis=1)
    draft_total = jnp.sum(jnp.exp(draft_logit), axis=1)
    label_logit = jnp.sum(jnp.where(is_label, draft_logit, 0.0), axis=1)
    draft_lse = jnp.log(draft_total)
    target_lse = jnp.log(target_total)
    row_loss = (
        draft_lse
        - (1.0 - label_mix) * cross_total / target_total
        - label_mix * label_logit
        + z_weight * draft_lse * draft_lse
    )
    logit_grad = (
        (
            (1.0 + 2.0 * z_weight * draft_lse)[:, None] * jnp.exp(draft_logit - draft_lse[:, None])
            - (1.0 - label_mix) * jnp.exp(target_logit - target_lse[:, None])
            - label_mix * is_label.astype(jnp.float32)
        )
    ).astype(jnp.bfloat16)

    send4 = jnp.broadcast_to(
        logit_grad.reshape(per_dev, 1, groups, vocab_tile).transpose(1, 2, 0, 3),
        (count_sec, groups, per_dev, vocab_tile),
    ).reshape(n_dev, per_dev, vocab_tile)
    grad_tile = exchange(send4, ALL).reshape(total_rows, vocab_tile)

    grad_part = jnp.dot(grad_tile, head, preferred_element_type=jnp.float32)
    loss_cols = jnp.pad(row_loss[:, None], ((0, 0), (0, 127)))
    send5 = jnp.concatenate(
        [
            grad_part.reshape(n_dev, per_dev, width),
            jnp.broadcast_to(loss_cols[None], (n_dev,) + loss_cols.shape),
        ],
        axis=2,
    )
    got5 = exchange(send5, ALL).reshape(count_sec, groups, per_dev, -1)
    draft_grad = (
        jnp.sum(got5[..., :width], axis=1).transpose(1, 0, 2).reshape(per_dev, full_width)
    )
    loss = jnp.mean(got5[..., width].reshape(total_rows))
    upstream = draft_grad * gain_full
    inner_sum = jnp.sum(hidden * upstream, axis=1)
    hidden_grad = (
        draft_scale[:, None] * upstream - hidden * (draft_scale**3 * inner_sum / D)[:, None]
    ).astype(jnp.bfloat16)

    send6 = jnp.broadcast_to(
        hidden_grad.reshape(per_dev, 1, groups, block).transpose(1, 2, 0, 3),
        (count_sec, groups, per_dev, block),
    ).reshape(n_dev, per_dev, block)
    block_grad = exchange(send6, ALL).reshape(total_rows, block)
    grad_embed = contract_first(embed_all, block_grad)
    grad_feature = contract_first(feature_all, block_grad)
    return (loss, grad_embed, grad_feature)


def solution(mesh):
    return jax.shard_map(
        on_device,
        mesh=mesh,
        in_specs=(
            P("dp", None, "section"),
            P("dp", None, "section"),
            P(),
            P(),
            P(),
            P("section"),
            P("section"),
            P(("mp", "dp"), "section"),
            P("section", ("mp", "dp")),
            P("section", ("mp", "dp")),
        ),
        out_specs=(P(), P("section", ("mp", "dp")), P("section", ("mp", "dp"))),
        check_vma=False,
    )
```

```python
import jax
import jax.numpy as jnp
from jax import lax
from jax.sharding import PartitionSpec as P

D = 8192
R_OWN = 8


z_weight = 0.004
label_mix = 0.1
eps_norm = 1e-05

ALL = ("section", "mp", "dp")


def contract_last(operand, weights):
    return lax.dot_general(
        operand, weights, (((1,), (1,)), ((), ())), preferred_element_type=jnp.float32
    )


def contract_first(operand, weights):
    return lax.dot_general(
        operand, weights, (((0,), (0,)), ((), ())), preferred_element_type=jnp.float32
    )


def locate(packed, starts, lengths, offsets):
    rel = packed[:, None] - starts[None, :]
    inside = (rel >= 0) & (rel < lengths[None, :])
    seq = jnp.sum(jnp.where(inside, jnp.arange(starts.shape[0], dtype=jnp.int32)[None, :], 0), axis=1)
    slot = jnp.sum(jnp.where(inside, rel, 0), axis=1)
    offset = jnp.sum(jnp.where(inside, offsets[None, :], 0), axis=1)
    return seq, slot, offset


def exchange(send, axes):
    return lax.all_to_all(send, axes, split_axis=0, concat_axis=0, tiled=True)


def shifted(x, axis):
    count = lax.axis_size(axis)
    parts = [x] + [
        lax.ppermute(x, axis, [(i, (i + k) % count) for i in range(count)])
        for k in range(1, count)
    ]
    return jnp.stack(parts)


def pad_cols(count):
    return -(-count // 128) * 128


def on_device(
    target_hidden,
    embeds,
    token_ids,
    lengths,
    offsets,
    target_gain,
    draft_gain,
    head,
    fc_embed,
    fc_feature,
):
    count_dp = lax.axis_size("dp")
    count_mp = lax.axis_size("mp")
    count_sec = lax.axis_size("section")
    groups = count_mp * count_dp
    n_dev = count_sec * groups
    my_dp = lax.axis_index("dp")
    my_mp = lax.axis_index("mp")
    my_sec = lax.axis_index("section")
    me = (my_sec * count_mp + my_mp) * count_dp + my_dp
    width = target_hidden.shape[2]
    seq_len = target_hidden.shape[1]
    vocab_tile = head.shape[0]
    block = fc_embed.shape[1]
    full_width = width * count_sec
    total_rows = R_OWN * groups
    per_dev = total_rows // n_dev
    half = 2 * R_OWN
    count_seq = lengths.shape[0]
    earlier = jnp.arange(count_seq)[None, :] < jnp.arange(count_seq)[:, None]
    starts = jnp.sum(jnp.where(earlier, lengths[None, :], 0), axis=1)

    first = jnp.minimum(offsets[my_dp] + my_mp * half, seq_len - half)
    mine = jnp.stack(
        [
            lax.dynamic_slice_in_dim(embeds[0], first, half, axis=0),
            lax.dynamic_slice_in_dim(target_hidden[0], first, half, axis=0),
        ]
    )
    every = shifted(shifted(mine, "dp"), "mp")
    every = every.transpose(2, 0, 1, 3, 4).reshape(2, count_mp * count_dp * half, width)
    packed = jnp.arange(total_rows, dtype=jnp.int32)
    seq_all, slot_all, offset_all = locate(packed, starts, lengths, offsets)
    shift_mp = (my_mp - slot_all // half) % count_mp
    shift_dp = (my_dp - seq_all) % count_dp
    base = offset_all + (slot_all // half) * half
    lag = base - jnp.minimum(base, seq_len - half)
    within = jnp.minimum(slot_all % half + lag, half - 1)
    pick = (shift_mp * count_dp + shift_dp) * half + within
    embed_all = jnp.take(every[0], pick, axis=0)
    feature_all = jnp.take(every[1], pick, axis=0)
    my_rows = me * per_dev + jnp.arange(per_dev, dtype=jnp.int32)
    my_seq, my_slot, my_offset = locate(my_rows, starts, lengths, offsets)
    flat = my_seq * seq_len + my_offset + my_slot
    ids = token_ids.reshape(-1)
    labels = jnp.sum(
        jnp.where(jnp.arange(ids.shape[0], dtype=jnp.int32)[None, :] == flat[:, None], ids, 0),
        axis=1,
    )

    partial_value = jnp.dot(embed_all, fc_embed, preferred_element_type=jnp.float32) + jnp.dot(
        feature_all, fc_feature, preferred_element_type=jnp.float32
    )
    target_square = jnp.sum(jnp.square(feature_all.astype(jnp.float32)), axis=1)
    piece = width // groups
    spare = pad_cols(-(-(total_rows + piece) // per_dev))
    gain_piece = lax.dynamic_slice_in_dim(draft_gain, (my_mp * count_dp + my_dp) * piece, piece)
    extra = jnp.pad(
        jnp.concatenate([target_square, gain_piece]),
        (0, per_dev * spare - total_rows - piece),
    ).reshape(per_dev, spare)
    send1 = jnp.concatenate(
        [
            partial_value.reshape(n_dev, per_dev, block),
            jnp.broadcast_to(extra[None], (n_dev,) + extra.shape),
        ],
        axis=2,
    )
    got1 = exchange(send1, ALL).reshape(count_sec, groups, per_dev, -1)
    hidden = (
        jnp.sum(got1[..., :block], axis=0).transpose(1, 0, 2).reshape(per_dev, groups * block)
    )
    extra_got = got1[..., block:].reshape(count_sec, groups, per_dev * spare)
    target_square = jnp.sum(extra_got[:, 0, :total_rows], axis=0)
    gain_full = extra_got[:, :, total_rows : total_rows + piece].reshape(full_width)
    target_scale = lax.rsqrt(target_square / D + eps_norm)
    target_norm = (feature_all.astype(jnp.float32) * target_scale[:, None] * target_gain).astype(
        jnp.bfloat16
    )
    draft_square = jnp.sum(hidden * hidden, axis=1)
    draft_scale = lax.rsqrt(draft_square / D + eps_norm)
    draft_norm = (hidden * draft_scale[:, None] * gain_full).astype(jnp.bfloat16)

    send2 = jnp.broadcast_to(
        draft_norm.reshape(per_dev, count_sec, 1, width).transpose(1, 2, 0, 3),
        (count_sec, groups, per_dev, width),
    ).reshape(n_dev, per_dev, width)
    draft_norm_all = exchange(send2, ALL).reshape(total_rows, width)

    target_part = contract_last(target_norm, head)
    draft_part = contract_last(draft_norm_all, head)
    send3 = jnp.stack([target_part, draft_part]).reshape(2, n_dev, per_dev, vocab_tile)
    got3 = lax.all_to_all(send3, ALL, split_axis=1, concat_axis=1, tiled=True)
    got3 = got3.reshape(2, count_sec, groups, per_dev, vocab_tile)
    logits = jnp.sum(got3, axis=1).transpose(0, 2, 1, 3).reshape(2, per_dev, groups * vocab_tile)
    target_logit, draft_logit = logits[0], logits[1]
    vocab = groups * vocab_tile
    is_label = labels[:, None] == jnp.arange(vocab, dtype=jnp.int32)[None, :]
    target_exp = jnp.exp(target_logit)
    target_total = jnp.sum(target_exp, axis=1)
    cross_total = jnp.sum(target_exp * draft_logit, axis=1)
    draft_total = jnp.sum(jnp.exp(draft_logit), axis=1)
    label_logit = jnp.sum(jnp.where(is_label, draft_logit, 0.0), axis=1)
    draft_lse = jnp.log(draft_total)
    target_lse = jnp.log(target_total)
    row_loss = (
        draft_lse
        - (1.0 - label_mix) * cross_total / target_total
        - label_mix * label_logit
        + z_weight * draft_lse * draft_lse
    )
    logit_grad = (
        (
            (1.0 + 2.0 * z_weight * draft_lse)[:, None] * jnp.exp(draft_logit - draft_lse[:, None])
            - (1.0 - label_mix) * jnp.exp(target_logit - target_lse[:, None])
            - label_mix * is_label.astype(jnp.float32)
        )
    ).astype(jnp.bfloat16)

    send4 = jnp.broadcast_to(
        logit_grad.reshape(per_dev, 1, groups, vocab_tile).transpose(1, 2, 0, 3),
        (count_sec, groups, per_dev, vocab_tile),
    ).reshape(n_dev, per_dev, vocab_tile)
    grad_tile = exchange(send4, ALL).reshape(total_rows, vocab_tile)

    grad_part = jnp.dot(grad_tile, head, preferred_element_type=jnp.float32)
    loss_cols = jnp.pad(row_loss[:, None], ((0, 0), (0, 127)))
    send5 = jnp.concatenate(
        [
            grad_part.reshape(n_dev, per_dev, width),
            jnp.broadcast_to(loss_cols[None], (n_dev,) + loss_cols.shape),
        ],
        axis=2,
    )
    got5 = exchange(send5, ALL).reshape(count_sec, groups, per_dev, -1)
    draft_grad = (
        jnp.sum(got5[..., :width], axis=1).transpose(1, 0, 2).reshape(per_dev, full_width)
    )
    loss = jnp.mean(got5[..., width].reshape(total_rows))
    upstream = draft_grad * gain_full
    inner_sum = jnp.sum(hidden * upstream, axis=1)
    hidden_grad = (
        draft_scale[:, None] * upstream - hidden * (draft_scale**3 * inner_sum / D)[:, None]
    ).astype(jnp.bfloat16)

    send6 = jnp.broadcast_to(
        hidden_grad.reshape(per_dev, 1, groups, block).transpose(1, 2, 0, 3),
        (count_sec, groups, per_dev, block),
    ).reshape(n_dev, per_dev, block)
    block_grad = exchange(send6, ALL).reshape(total_rows, block)
    grad_embed = contract_first(embed_all, block_grad)
    grad_feature = contract_first(feature_all, block_grad)
    return (loss, grad_embed, grad_feature)


def solution(mesh):
    return jax.shard_map(
        on_device,
        mesh=mesh,
        in_specs=(
            P("dp", None, "section"),
            P("dp", None, "section"),
            P(),
            P(),
            P(),
            P("section"),
            P("section"),
            P(("mp", "dp"), "section"),
            P("section", ("mp", "dp")),
            P("section", ("mp", "dp")),
        ),
        out_specs=(P(), P("section", ("mp", "dp")), P("section", ("mp", "dp"))),
        check_vma=False,
    )
```

```python
import jax
import jax.numpy as jnp
from jax import lax
from jax.sharding import PartitionSpec as P

D = 8192
R_OWN = 8


z_weight = 0.004
label_mix = 0.1
eps_norm = 1e-05

ALL = ("section", "mp", "dp")


def contract_last(operand, weights):
    return lax.dot_general(
        operand, weights, (((1,), (1,)), ((), ())), preferred_element_type=jnp.float32
    )


def contract_first(operand, weights):
    return lax.dot_general(
        operand, weights, (((0,), (0,)), ((), ())), preferred_element_type=jnp.float32
    )


def locate(packed, starts, lengths, offsets):
    rel = packed[:, None] - starts[None, :]
    inside = (rel >= 0) & (rel < lengths[None, :])
    seq = jnp.sum(jnp.where(inside, jnp.arange(starts.shape[0], dtype=jnp.int32)[None, :], 0), axis=1)
    slot = jnp.sum(jnp.where(inside, rel, 0), axis=1)
    offset = jnp.sum(jnp.where(inside, offsets[None, :], 0), axis=1)
    return seq, slot, offset


def exchange(send, axes):
    return lax.all_to_all(send, axes, split_axis=0, concat_axis=0, tiled=True)


def shifted(x, axis):
    count = lax.axis_size(axis)
    parts = [x] + [
        lax.ppermute(x, axis, [(i, (i + k) % count) for i in range(count)])
        for k in range(1, count)
    ]
    return jnp.stack(parts)


def pad_cols(count):
    return -(-count // 128) * 128


def on_device(
    target_hidden,
    embeds,
    token_ids,
    lengths,
    offsets,
    target_gain,
    draft_gain,
    head,
    fc_embed,
    fc_feature,
):
    count_dp = lax.axis_size("dp")
    count_mp = lax.axis_size("mp")
    count_sec = lax.axis_size("section")
    groups = count_mp * count_dp
    n_dev = count_sec * groups
    my_dp = lax.axis_index("dp")
    my_mp = lax.axis_index("mp")
    my_sec = lax.axis_index("section")
    me = (my_sec * count_mp + my_mp) * count_dp + my_dp
    width = target_hidden.shape[2]
    seq_len = target_hidden.shape[1]
    vocab_tile = head.shape[0]
    block = fc_embed.shape[1]
    full_width = width * count_sec
    total_rows = R_OWN * groups
    per_dev = total_rows // n_dev
    half = 2 * R_OWN
    count_seq = lengths.shape[0]
    earlier = jnp.arange(count_seq)[None, :] < jnp.arange(count_seq)[:, None]
    starts = jnp.sum(jnp.where(earlier, lengths[None, :], 0), axis=1)

    first = jnp.minimum(offsets[my_dp] + my_mp * half, seq_len - half)
    mine = jnp.stack(
        [
            lax.dynamic_slice_in_dim(embeds[0], first, half, axis=0),
            lax.dynamic_slice_in_dim(target_hidden[0], first, half, axis=0),
        ]
    )
    every = shifted(shifted(mine, "dp"), "mp")
    every = every.transpose(2, 0, 1, 3, 4).reshape(2, count_mp * count_dp * half, width)
    packed = jnp.arange(total_rows, dtype=jnp.int32)
    seq_all, slot_all, offset_all = locate(packed, starts, lengths, offsets)
    shift_mp = (my_mp - slot_all // half) % count_mp
    shift_dp = (my_dp - seq_all) % count_dp
    base = offset_all + (slot_all // half) * half
    lag = base - jnp.minimum(base, seq_len - half)
    within = jnp.minimum(slot_all % half + lag, half - 1)
    pick = (shift_mp * count_dp + shift_dp) * half + within
    embed_all = jnp.take(every[0], pick, axis=0)
    feature_all = jnp.take(every[1], pick, axis=0)
    my_rows = me * per_dev + jnp.arange(per_dev, dtype=jnp.int32)
    my_seq, my_slot, my_offset = locate(my_rows, starts, lengths, offsets)
    flat = my_seq * seq_len + my_offset + my_slot
    ids = token_ids.reshape(-1)
    labels = jnp.sum(
        jnp.where(jnp.arange(ids.shape[0], dtype=jnp.int32)[None, :] == flat[:, None], ids, 0),
        axis=1,
    )

    partial_value = jnp.dot(embed_all, fc_embed, preferred_element_type=jnp.float32) + jnp.dot(
        feature_all, fc_feature, preferred_element_type=jnp.float32
    )
    target_square = jnp.sum(jnp.square(feature_all.astype(jnp.float32)), axis=1)
    piece = width // groups
    spare = pad_cols(-(-(total_rows + piece) // per_dev))
    gain_piece = lax.dynamic_slice_in_dim(draft_gain, (my_mp * count_dp + my_dp) * piece, piece)
    extra = jnp.pad(
        jnp.concatenate([target_square, gain_piece]),
        (0, per_dev * spare - total_rows - piece),
    ).reshape(per_dev, spare)
    send1 = jnp.concatenate(
        [
            partial_value.reshape(n_dev, per_dev, block),
            jnp.broadcast_to(extra[None], (n_dev,) + extra.shape),
        ],
        axis=2,
    )
    got1 = exchange(send1, ALL).reshape(count_sec, groups, per_dev, -1)
    hidden = (
        jnp.sum(got1[..., :block], axis=0).transpose(1, 0, 2).reshape(per_dev, groups * block)
    )
    extra_got = got1[..., block:].reshape(count_sec, groups, per_dev * spare)
    target_square = jnp.sum(extra_got[:, 0, :total_rows], axis=0)
    gain_full = extra_got[:, :, total_rows : total_rows + piece].reshape(full_width)
    target_scale = lax.rsqrt(target_square / D + eps_norm)
    target_norm = (feature_all.astype(jnp.float32) * target_scale[:, None] * target_gain).astype(
        jnp.bfloat16
    )
    draft_square = jnp.sum(hidden * hidden, axis=1)
    draft_scale = lax.rsqrt(draft_square / D + eps_norm)
    draft_norm = (hidden * draft_scale[:, None] * gain_full).astype(jnp.bfloat16)

    send2 = jnp.broadcast_to(
        draft_norm.reshape(per_dev, count_sec, 1, width).transpose(1, 2, 0, 3),
        (count_sec, groups, per_dev, width),
    ).reshape(n_dev, per_dev, width)
    draft_norm_all = exchange(send2, ALL).reshape(total_rows, width)

    target_part = contract_last(target_norm, head)
    draft_part = contract_last(draft_norm_all, head)
    send3 = jnp.stack([target_part, draft_part]).reshape(2, n_dev, per_dev, vocab_tile)
    got3 = lax.all_to_all(send3, ALL, split_axis=1, concat_axis=1, tiled=True)
    got3 = got3.reshape(2, count_sec, groups, per_dev, vocab_tile)
    logits = jnp.sum(got3, axis=1).transpose(0, 2, 1, 3).reshape(2, per_dev, groups * vocab_tile)
    target_logit, draft_logit = logits[0], logits[1]
    vocab = groups * vocab_tile
    is_label = labels[:, None] == jnp.arange(vocab, dtype=jnp.int32)[None, :]
    target_exp = jnp.exp(target_logit)
    target_total = jnp.sum(target_exp, axis=1)
    cross_total = jnp.sum(target_exp * draft_logit, axis=1)
    draft_total = jnp.sum(jnp.exp(draft_logit), axis=1)
    label_logit = jnp.sum(jnp.where(is_label, draft_logit, 0.0), axis=1)
    draft_lse = jnp.log(draft_total)
    target_lse = jnp.log(target_total)
    row_loss = (
        draft_lse
        - (1.0 - label_mix) * cross_total / target_total
        - label_mix * label_logit
        + z_weight * draft_lse * draft_lse
    )
    logit_grad = (
        (
            (1.0 + 2.0 * z_weight * draft_lse)[:, None] * jnp.exp(draft_logit - draft_lse[:, None])
            - (1.0 - label_mix) * jnp.exp(target_logit - target_lse[:, None])
            - label_mix * is_label.astype(jnp.float32)
        )
    ).astype(jnp.bfloat16)

    send4 = jnp.broadcast_to(
        logit_grad.reshape(per_dev, 1, groups, vocab_tile).transpose(1, 2, 0, 3),
        (count_sec, groups, per_dev, vocab_tile),
    ).reshape(n_dev, per_dev, vocab_tile)
    grad_tile = exchange(send4, ALL).reshape(total_rows, vocab_tile)

    grad_part = jnp.dot(grad_tile, head, preferred_element_type=jnp.float32)
    by_mp = grad_part.reshape(count_sec, count_mp, count_dp, per_dev, width).transpose(1, 0, 2, 3, 4)
    loss_cols = jnp.broadcast_to(
        jnp.pad(row_loss[:, None], ((0, 0), (0, 127))), (count_sec, count_dp, per_dev, 128)
    )
    got_mp = []
    for k in range(count_mp):
        payload = jnp.concatenate(
            [lax.dynamic_index_in_dim(by_mp, (my_mp + k) % count_mp, 0, keepdims=False), loss_cols],
            axis=3,
        )
        if k:
            payload = lax.ppermute(payload, "mp", [(i, (i + k) % count_mp) for i in range(count_mp)])
        got_mp.append(payload)
    got_mp = jnp.stack(got_mp)
    reduced = jnp.sum(got_mp[..., :width], axis=0)
    pair = jnp.take(
        got_mp[:, 0, 0, :, width], (my_mp - jnp.arange(count_mp, dtype=jnp.int32)) % count_mp, axis=0
    )
    pair_cols = jnp.broadcast_to(
        jnp.pad(pair.T, ((0, 0), (0, 128 - count_mp))), (count_sec, count_dp, per_dev, 128)
    )
    send5 = jnp.concatenate([reduced, pair_cols], axis=3).reshape(
        count_sec * count_dp, per_dev, width + 128
    )
    got5 = exchange(send5, ("section", "dp")).reshape(count_sec, count_dp, per_dev, width + 128)
    draft_grad = (
        jnp.sum(got5[..., :width], axis=1).transpose(1, 0, 2).reshape(per_dev, full_width)
    )
    loss = jnp.mean(got5[..., width : width + count_mp])
    upstream = draft_grad * gain_full
    inner_sum = jnp.sum(hidden * upstream, axis=1)
    hidden_grad = (
        draft_scale[:, None] * upstream - hidden * (draft_scale**3 * inner_sum / D)[:, None]
    ).astype(jnp.bfloat16)

    send6 = jnp.broadcast_to(
        hidden_grad.reshape(per_dev, 1, groups, block).transpose(1, 2, 0, 3),
        (count_sec, groups, per_dev, block),
    ).reshape(n_dev, per_dev, block)
    block_grad = exchange(send6, ALL).reshape(total_rows, block)
    grad_embed = contract_first(embed_all, block_grad)
    grad_feature = contract_first(feature_all, block_grad)
    return (loss, grad_embed, grad_feature)


def solution(mesh):
    return jax.shard_map(
        on_device,
        mesh=mesh,
        in_specs=(
            P("dp", None, "section"),
            P("dp", None, "section"),
            P(),
            P(),
            P(),
            P("section"),
            P("section"),
            P(("mp", "dp"), "section"),
            P("section", ("mp", "dp")),
            P("section", ("mp", "dp")),
        ),
        out_specs=(P(), P("section", ("mp", "dp")), P("section", ("mp", "dp"))),
        check_vma=False,
    )
```

```python
import jax
import jax.numpy as jnp
from jax import lax
from jax.sharding import PartitionSpec as P

D = 8192
R_OWN = 8


z_weight = 0.004
label_mix = 0.1
eps_norm = 1e-05

ALL = ("section", "mp", "dp")


def contract_last(operand, weights):
    return lax.dot_general(
        operand, weights, (((1,), (1,)), ((), ())), preferred_element_type=jnp.float32
    )


def contract_first(operand, weights):
    return lax.dot_general(
        operand, weights, (((0,), (0,)), ((), ())), preferred_element_type=jnp.float32
    )


def locate(packed, starts, lengths, offsets):
    rel = packed[:, None] - starts[None, :]
    inside = (rel >= 0) & (rel < lengths[None, :])
    seq = jnp.sum(jnp.where(inside, jnp.arange(starts.shape[0], dtype=jnp.int32)[None, :], 0), axis=1)
    slot = jnp.sum(jnp.where(inside, rel, 0), axis=1)
    offset = jnp.sum(jnp.where(inside, offsets[None, :], 0), axis=1)
    return seq, slot, offset


def exchange(send, axes):
    return lax.all_to_all(send, axes, split_axis=0, concat_axis=0, tiled=True)


def shifted(x, axis):
    count = lax.axis_size(axis)
    parts = [x] + [
        lax.ppermute(x, axis, [(i, (i + k) % count) for i in range(count)])
        for k in range(1, count)
    ]
    return jnp.stack(parts)


def pad_cols(count):
    return -(-count // 128) * 128


def on_device(
    target_hidden,
    embeds,
    token_ids,
    lengths,
    offsets,
    target_gain,
    draft_gain,
    head,
    fc_embed,
    fc_feature,
):
    count_dp = lax.axis_size("dp")
    count_mp = lax.axis_size("mp")
    count_sec = lax.axis_size("section")
    groups = count_mp * count_dp
    n_dev = count_sec * groups
    my_dp = lax.axis_index("dp")
    my_mp = lax.axis_index("mp")
    my_sec = lax.axis_index("section")
    me = (my_sec * count_mp + my_mp) * count_dp + my_dp
    width = target_hidden.shape[2]
    seq_len = target_hidden.shape[1]
    vocab_tile = head.shape[0]
    block = fc_embed.shape[1]
    full_width = width * count_sec
    total_rows = R_OWN * groups
    per_dev = total_rows // n_dev
    half = 2 * R_OWN
    count_seq = lengths.shape[0]
    earlier = jnp.arange(count_seq)[None, :] < jnp.arange(count_seq)[:, None]
    starts = jnp.sum(jnp.where(earlier, lengths[None, :], 0), axis=1)

    cap = half * count_mp
    first = jnp.minimum(offsets[my_dp], seq_len - cap)
    mine = jnp.stack(
        [
            lax.dynamic_slice_in_dim(embeds[0], first, cap, axis=0),
            lax.dynamic_slice_in_dim(target_hidden[0], first, cap, axis=0),
        ]
    )
    every = shifted(mine, "dp")
    every = every.transpose(1, 0, 2, 3).reshape(2, count_dp * cap, width)
    packed = jnp.arange(total_rows, dtype=jnp.int32)
    seq_all, slot_all, offset_all = locate(packed, starts, lengths, offsets)
    shift_dp = (my_dp - seq_all) % count_dp
    lag = offset_all - jnp.minimum(offset_all, seq_len - cap)
    within = jnp.minimum(slot_all + lag, cap - 1)
    pick = shift_dp * cap + within
    embed_all = jnp.take(every[0], pick, axis=0)
    feature_all = jnp.take(every[1], pick, axis=0)
    my_rows = me * per_dev + jnp.arange(per_dev, dtype=jnp.int32)
    my_seq, my_slot, my_offset = locate(my_rows, starts, lengths, offsets)
    flat = my_seq * seq_len + my_offset + my_slot
    ids = token_ids.reshape(-1)
    labels = jnp.sum(
        jnp.where(jnp.arange(ids.shape[0], dtype=jnp.int32)[None, :] == flat[:, None], ids, 0),
        axis=1,
    )

    partial_value = jnp.dot(embed_all, fc_embed, preferred_element_type=jnp.float32) + jnp.dot(
        feature_all, fc_feature, preferred_element_type=jnp.float32
    )
    target_square = jnp.sum(jnp.square(feature_all.astype(jnp.float32)), axis=1)
    piece = width // groups
    spare = pad_cols(-(-(total_rows + piece) // per_dev))
    gain_piece = lax.dynamic_slice_in_dim(draft_gain, (my_mp * count_dp + my_dp) * piece, piece)
    extra = jnp.pad(
        jnp.concatenate([target_square, gain_piece]),
        (0, per_dev * spare - total_rows - piece),
    ).reshape(per_dev, spare)
    send1 = jnp.concatenate(
        [
            partial_value.reshape(n_dev, per_dev, block),
            jnp.broadcast_to(extra[None], (n_dev,) + extra.shape),
        ],
        axis=2,
    )
    got1 = exchange(send1, ALL).reshape(count_sec, groups, per_dev, -1)
    hidden = (
        jnp.sum(got1[..., :block], axis=0).transpose(1, 0, 2).reshape(per_dev, groups * block)
    )
    extra_got = got1[..., block:].reshape(count_sec, groups, per_dev * spare)
    target_square = jnp.sum(extra_got[:, 0, :total_rows], axis=0)
    gain_full = extra_got[:, :, total_rows : total_rows + piece].reshape(full_width)
    target_scale = lax.rsqrt(target_square / D + eps_norm)
    target_norm = (feature_all.astype(jnp.float32) * target_scale[:, None] * target_gain).astype(
        jnp.bfloat16
    )
    draft_square = jnp.sum(hidden * hidden, axis=1)
    draft_scale = lax.rsqrt(draft_square / D + eps_norm)
    draft_norm = (hidden * draft_scale[:, None] * gain_full).astype(jnp.bfloat16)

    send2 = jnp.broadcast_to(
        draft_norm.reshape(per_dev, count_sec, 1, width).transpose(1, 2, 0, 3),
        (count_sec, groups, per_dev, width),
    ).reshape(n_dev, per_dev, width)
    draft_norm_all = exchange(send2, ALL).reshape(total_rows, width)

    target_part = contract_last(target_norm, head)
    draft_part = contract_last(draft_norm_all, head)
    send3 = jnp.stack([target_part, draft_part]).reshape(2, n_dev, per_dev, vocab_tile)
    got3 = lax.all_to_all(send3, ALL, split_axis=1, concat_axis=1, tiled=True)
    got3 = got3.reshape(2, count_sec, groups, per_dev, vocab_tile)
    logits = jnp.sum(got3, axis=1).transpose(0, 2, 1, 3).reshape(2, per_dev, groups * vocab_tile)
    target_logit, draft_logit = logits[0], logits[1]
    vocab = groups * vocab_tile
    is_label = labels[:, None] == jnp.arange(vocab, dtype=jnp.int32)[None, :]
    target_exp = jnp.exp(target_logit)
    target_total = jnp.sum(target_exp, axis=1)
    cross_total = jnp.sum(target_exp * draft_logit, axis=1)
    draft_total = jnp.sum(jnp.exp(draft_logit), axis=1)
    label_logit = jnp.sum(jnp.where(is_label, draft_logit, 0.0), axis=1)
    draft_lse = jnp.log(draft_total)
    target_lse = jnp.log(target_total)
    row_loss = (
        draft_lse
        - (1.0 - label_mix) * cross_total / target_total
        - label_mix * label_logit
        + z_weight * draft_lse * draft_lse
    )
    logit_grad = (
        (
            (1.0 + 2.0 * z_weight * draft_lse)[:, None] * jnp.exp(draft_logit - draft_lse[:, None])
            - (1.0 - label_mix) * jnp.exp(target_logit - target_lse[:, None])
            - label_mix * is_label.astype(jnp.float32)
        )
    ).astype(jnp.bfloat16)

    send4 = jnp.broadcast_to(
        logit_grad.reshape(per_dev, 1, groups, vocab_tile).transpose(1, 2, 0, 3),
        (count_sec, groups, per_dev, vocab_tile),
    ).reshape(n_dev, per_dev, vocab_tile)
    grad_tile = exchange(send4, ALL).reshape(total_rows, vocab_tile)

    grad_part = jnp.dot(grad_tile, head, preferred_element_type=jnp.float32)
    by_mp = grad_part.reshape(count_sec, count_mp, count_dp, per_dev, width).transpose(1, 0, 2, 3, 4)
    loss_cols = jnp.broadcast_to(
        jnp.pad(row_loss[:, None], ((0, 0), (0, 127))), (count_sec, count_dp, per_dev, 128)
    )
    got_mp = []
    for k in range(count_mp):
        payload = jnp.concatenate(
            [lax.dynamic_index_in_dim(by_mp, (my_mp + k) % count_mp, 0, keepdims=False), loss_cols],
            axis=3,
        )
        if k:
            payload = lax.ppermute(payload, "mp", [(i, (i + k) % count_mp) for i in range(count_mp)])
        got_mp.append(payload)
    got_mp = jnp.stack(got_mp)
    reduced = jnp.sum(got_mp[..., :width], axis=0)
    pair = jnp.take(
        got_mp[:, 0, 0, :, width], (my_mp - jnp.arange(count_mp, dtype=jnp.int32)) % count_mp, axis=0
    )
    pair_cols = jnp.broadcast_to(
        jnp.pad(pair.T, ((0, 0), (0, 128 - count_mp))), (count_sec, count_dp, per_dev, 128)
    )
    send5 = jnp.concatenate([reduced, pair_cols], axis=3).reshape(
        count_sec * count_dp, per_dev, width + 128
    )
    got5 = exchange(send5, ("section", "dp")).reshape(count_sec, count_dp, per_dev, width + 128)
    draft_grad = (
        jnp.sum(got5[..., :width], axis=1).transpose(1, 0, 2).reshape(per_dev, full_width)
    )
    loss = jnp.mean(got5[..., width : width + count_mp])
    upstream = draft_grad * gain_full
    inner_sum = jnp.sum(hidden * upstream, axis=1)
    hidden_grad = (
        draft_scale[:, None] * upstream - hidden * (draft_scale**3 * inner_sum / D)[:, None]
    ).astype(jnp.bfloat16)

    send6 = jnp.broadcast_to(
        hidden_grad.reshape(per_dev, 1, groups, block).transpose(1, 2, 0, 3),
        (count_sec, groups, per_dev, block),
    ).reshape(n_dev, per_dev, block)
    block_grad = exchange(send6, ALL).reshape(total_rows, block)
    grad_embed = contract_first(embed_all, block_grad)
    grad_feature = contract_first(feature_all, block_grad)
    return (loss, grad_embed, grad_feature)


def solution(mesh):
    return jax.shard_map(
        on_device,
        mesh=mesh,
        in_specs=(
            P("dp", None, "section"),
            P("dp", None, "section"),
            P(),
            P(),
            P(),
            P("section"),
            P("section"),
            P(("mp", "dp"), "section"),
            P("section", ("mp", "dp")),
            P("section", ("mp", "dp")),
        ),
        out_specs=(P(), P("section", ("mp", "dp")), P("section", ("mp", "dp"))),
        check_vma=False,
    )
```

```python
import jax
import jax.numpy as jnp
from jax import lax
from jax.sharding import PartitionSpec as P

D = 8192
R_OWN = 8


z_weight = 0.004
label_mix = 0.1
eps_norm = 1e-05

ALL = ("section", "mp", "dp")


def contract_last(operand, weights):
    return lax.dot_general(
        operand, weights, (((1,), (1,)), ((), ())), preferred_element_type=jnp.float32
    )


def contract_first(operand, weights):
    return lax.dot_general(
        operand, weights, (((0,), (0,)), ((), ())), preferred_element_type=jnp.float32
    )


def locate(packed, starts, lengths, offsets):
    rel = packed[:, None] - starts[None, :]
    inside = (rel >= 0) & (rel < lengths[None, :])
    seq = jnp.sum(jnp.where(inside, jnp.arange(starts.shape[0], dtype=jnp.int32)[None, :], 0), axis=1)
    slot = jnp.sum(jnp.where(inside, rel, 0), axis=1)
    offset = jnp.sum(jnp.where(inside, offsets[None, :], 0), axis=1)
    return seq, slot, offset


def exchange(send, axes):
    return lax.all_to_all(send, axes, split_axis=0, concat_axis=0, tiled=True)


def shifted(x, axis):
    count = lax.axis_size(axis)
    parts = [x] + [
        lax.ppermute(x, axis, [(i, (i + k) % count) for i in range(count)])
        for k in range(1, count)
    ]
    return jnp.stack(parts)


def section_sum(x):
    count = lax.axis_size("section")
    if count & (count - 1):
        mine = lax.axis_index("section")
        parts = jnp.stack(
            [x]
            + [
                lax.ppermute(x, "section", [(i, (i + k) % count) for i in range(count)])
                for k in range(1, count)
            ]
        )
        return jnp.sum(jnp.take(parts, (mine - jnp.arange(count)) % count, axis=0), axis=0)
    parts = [x] + [
        lax.ppermute(x, "section", [(i, i ^ k) for i in range(count)]) for k in range(1, count)
    ]
    while len(parts) > 1:
        parts = [parts[i] + parts[i + 1] for i in range(0, len(parts), 2)]
    return parts[0]


def pad_cols(count):
    return -(-count // 128) * 128


def on_device(
    target_hidden,
    embeds,
    token_ids,
    lengths,
    offsets,
    target_gain,
    draft_gain,
    head,
    fc_embed,
    fc_feature,
):
    count_dp = lax.axis_size("dp")
    count_mp = lax.axis_size("mp")
    count_sec = lax.axis_size("section")
    groups = count_mp * count_dp
    n_dev = count_sec * groups
    my_dp = lax.axis_index("dp")
    my_mp = lax.axis_index("mp")
    my_sec = lax.axis_index("section")
    me = (my_sec * count_mp + my_mp) * count_dp + my_dp
    width = target_hidden.shape[2]
    seq_len = target_hidden.shape[1]
    vocab_tile = head.shape[0]
    block = fc_embed.shape[1]
    full_width = width * count_sec
    total_rows = R_OWN * groups
    per_dev = total_rows // n_dev
    half = 2 * R_OWN
    count_seq = lengths.shape[0]
    earlier = jnp.arange(count_seq)[None, :] < jnp.arange(count_seq)[:, None]
    starts = jnp.sum(jnp.where(earlier, lengths[None, :], 0), axis=1)

    first = jnp.minimum(offsets[my_dp] + my_mp * half, seq_len - half)
    mine = jnp.stack(
        [
            lax.dynamic_slice_in_dim(embeds[0], first, half, axis=0),
            lax.dynamic_slice_in_dim(target_hidden[0], first, half, axis=0),
        ]
    )
    every = shifted(shifted(mine, "dp"), "mp")
    every = every.transpose(2, 0, 1, 3, 4).reshape(2, count_mp * count_dp * half, width)
    packed = jnp.arange(total_rows, dtype=jnp.int32)
    seq_all, slot_all, offset_all = locate(packed, starts, lengths, offsets)
    shift_mp = (my_mp - slot_all // half) % count_mp
    shift_dp = (my_dp - seq_all) % count_dp
    base = offset_all + (slot_all // half) * half
    lag = base - jnp.minimum(base, seq_len - half)
    within = jnp.minimum(slot_all % half + lag, half - 1)
    pick = (shift_mp * count_dp + shift_dp) * half + within
    embed_all = jnp.take(every[0], pick, axis=0)
    feature_all = jnp.take(every[1], pick, axis=0)
    flat = seq_all * seq_len + offset_all + slot_all
    ids = token_ids.reshape(-1)
    labels_all = jnp.sum(
        jnp.where(jnp.arange(ids.shape[0], dtype=jnp.int32)[None, :] == flat[:, None], ids, 0),
        axis=1,
    )

    partial_value = jnp.dot(embed_all, fc_embed, preferred_element_type=jnp.float32) + jnp.dot(
        feature_all, fc_feature, preferred_element_type=jnp.float32
    )
    target_square = jnp.sum(jnp.square(feature_all.astype(jnp.float32)), axis=1)
    piece = width // groups
    spare = pad_cols(-(-(total_rows + piece) // per_dev))
    gain_piece = lax.dynamic_slice_in_dim(draft_gain, (my_mp * count_dp + my_dp) * piece, piece)
    extra = jnp.pad(
        jnp.concatenate([target_square, gain_piece]),
        (0, per_dev * spare - total_rows - piece),
    ).reshape(per_dev, spare)
    send1 = jnp.concatenate(
        [
            partial_value.reshape(n_dev, per_dev, block),
            jnp.broadcast_to(extra[None], (n_dev,) + extra.shape),
        ],
        axis=2,
    )
    got1 = exchange(send1, ALL).reshape(count_sec, groups, per_dev, -1)
    hidden = (
        jnp.sum(got1[..., :block], axis=0).transpose(1, 0, 2).reshape(per_dev, groups * block)
    )
    extra_got = got1[..., block:].reshape(count_sec, groups, per_dev * spare)
    target_square = jnp.sum(extra_got[:, 0, :total_rows], axis=0)
    gain_full = extra_got[:, :, total_rows : total_rows + piece].reshape(full_width)
    target_scale = lax.rsqrt(target_square / D + eps_norm)
    target_norm = (feature_all.astype(jnp.float32) * target_scale[:, None] * target_gain).astype(
        jnp.bfloat16
    )
    draft_square = jnp.sum(hidden * hidden, axis=1)
    draft_scale = lax.rsqrt(draft_square / D + eps_norm)
    draft_norm = (hidden * draft_scale[:, None] * gain_full).astype(jnp.bfloat16)

    send2 = jnp.broadcast_to(
        draft_norm.reshape(per_dev, count_sec, 1, width).transpose(1, 2, 0, 3),
        (count_sec, groups, per_dev, width),
    ).reshape(n_dev, per_dev, width)
    draft_norm_all = exchange(send2, ALL).reshape(total_rows, width)

    target_logit = section_sum(contract_last(target_norm, head))
    draft_logit = section_sum(contract_last(draft_norm_all, head))
    column_zero = (my_mp * count_dp + my_dp) * vocab_tile
    is_label = (
        labels_all[:, None] - column_zero == jnp.arange(vocab_tile, dtype=jnp.int32)[None, :]
    )
    target_exp = jnp.exp(target_logit)
    sums = jnp.stack(
        [
            jnp.sum(target_exp, axis=1),
            jnp.sum(target_exp * draft_logit, axis=1),
            jnp.sum(jnp.exp(draft_logit), axis=1),
            jnp.sum(jnp.where(is_label, draft_logit, 0.0), axis=1),
        ]
    )
    sums = jnp.sum(
        exchange(jnp.broadcast_to(sums[None], (groups,) + sums.shape), ("mp", "dp")), axis=0
    )
    target_total, cross_total, draft_total, label_logit = sums[0], sums[1], sums[2], sums[3]
    draft_lse = jnp.log(draft_total)
    target_lse = jnp.log(target_total)
    row_loss = (
        draft_lse
        - (1.0 - label_mix) * cross_total / target_total
        - label_mix * label_logit
        + z_weight * draft_lse * draft_lse
    )
    loss = jnp.mean(row_loss)
    grad_tile = (
        (
            (1.0 + 2.0 * z_weight * draft_lse)[:, None] * jnp.exp(draft_logit - draft_lse[:, None])
            - (1.0 - label_mix) * jnp.exp(target_logit - target_lse[:, None])
            - label_mix * is_label.astype(jnp.float32)
        )
    ).astype(jnp.bfloat16)

    grad_part = jnp.dot(grad_tile, head, preferred_element_type=jnp.float32)
    by_mp = grad_part.reshape(count_sec, count_mp, count_dp, per_dev, width).transpose(1, 0, 2, 3, 4)
    reduced = lax.dynamic_index_in_dim(by_mp, my_mp, 0, keepdims=False)
    for k in range(1, count_mp):
        reduced = reduced + lax.ppermute(
            lax.dynamic_index_in_dim(by_mp, (my_mp + k) % count_mp, 0, keepdims=False),
            "mp",
            [(i, (i + k) % count_mp) for i in range(count_mp)],
        )
    send5 = reduced.reshape(count_sec * count_dp, per_dev, width)
    got5 = exchange(send5, ("section", "dp")).reshape(count_sec, count_dp, per_dev, width)
    draft_grad = jnp.sum(got5, axis=1).transpose(1, 0, 2).reshape(per_dev, full_width)
    upstream = draft_grad * gain_full
    inner_sum = jnp.sum(hidden * upstream, axis=1)
    hidden_grad = (
        draft_scale[:, None] * upstream - hidden * (draft_scale**3 * inner_sum / D)[:, None]
    ).astype(jnp.bfloat16)

    send6 = jnp.broadcast_to(
        hidden_grad.reshape(per_dev, 1, groups, block).transpose(1, 2, 0, 3),
        (count_sec, groups, per_dev, block),
    ).reshape(n_dev, per_dev, block)
    block_grad = exchange(send6, ALL).reshape(total_rows, block)
    grad_embed = contract_first(embed_all, block_grad)
    grad_feature = contract_first(feature_all, block_grad)
    return (loss, grad_embed, grad_feature)


def solution(mesh):
    return jax.shard_map(
        on_device,
        mesh=mesh,
        in_specs=(
            P("dp", None, "section"),
            P("dp", None, "section"),
            P(),
            P(),
            P(),
            P("section"),
            P("section"),
            P(("mp", "dp"), "section"),
            P("section", ("mp", "dp")),
            P("section", ("mp", "dp")),
        ),
        out_specs=(P(), P("section", ("mp", "dp")), P("section", ("mp", "dp"))),
        check_vma=False,
    )
```

```python
import jax
import jax.numpy as jnp
from jax import lax
from jax.sharding import PartitionSpec as P

D = 8192
R_OWN = 8


z_weight = 0.004
label_mix = 0.1
eps_norm = 1e-05

ALL = ("section", "mp", "dp")


def contract_last(operand, weights):
    return lax.dot_general(
        operand, weights, (((1,), (1,)), ((), ())), preferred_element_type=jnp.float32
    )


def contract_first(operand, weights):
    return lax.dot_general(
        operand, weights, (((0,), (0,)), ((), ())), preferred_element_type=jnp.float32
    )


def locate(packed, starts, lengths, offsets):
    rel = packed[:, None] - starts[None, :]
    inside = (rel >= 0) & (rel < lengths[None, :])
    seq = jnp.sum(jnp.where(inside, jnp.arange(starts.shape[0], dtype=jnp.int32)[None, :], 0), axis=1)
    slot = jnp.sum(jnp.where(inside, rel, 0), axis=1)
    offset = jnp.sum(jnp.where(inside, offsets[None, :], 0), axis=1)
    return seq, slot, offset


def exchange(send, axes):
    return lax.all_to_all(send, axes, split_axis=0, concat_axis=0, tiled=True)


def shifted(x, axis):
    count = lax.axis_size(axis)
    parts = [x] + [
        lax.ppermute(x, axis, [(i, (i + k) % count) for i in range(count)])
        for k in range(1, count)
    ]
    return jnp.stack(parts)


def section_sum(x):
    count = lax.axis_size("section")
    if count & (count - 1):
        mine = lax.axis_index("section")
        parts = jnp.stack(
            [x]
            + [
                lax.ppermute(x, "section", [(i, (i + k) % count) for i in range(count)])
                for k in range(1, count)
            ]
        )
        return jnp.sum(jnp.take(parts, (mine - jnp.arange(count)) % count, axis=0), axis=0)
    step = 1
    while step < count:
        x = x + lax.ppermute(x, "section", [(i, i ^ step) for i in range(count)])
        step *= 2
    return x


def pad_cols(count):
    return -(-count // 128) * 128


def on_device(
    target_hidden,
    embeds,
    token_ids,
    lengths,
    offsets,
    target_gain,
    draft_gain,
    head,
    fc_embed,
    fc_feature,
):
    count_dp = lax.axis_size("dp")
    count_mp = lax.axis_size("mp")
    count_sec = lax.axis_size("section")
    groups = count_mp * count_dp
    n_dev = count_sec * groups
    my_dp = lax.axis_index("dp")
    my_mp = lax.axis_index("mp")
    my_sec = lax.axis_index("section")
    me = (my_sec * count_mp + my_mp) * count_dp + my_dp
    width = target_hidden.shape[2]
    seq_len = target_hidden.shape[1]
    vocab_tile = head.shape[0]
    block = fc_embed.shape[1]
    full_width = width * count_sec
    total_rows = R_OWN * groups
    per_dev = total_rows // n_dev
    half = 2 * R_OWN
    count_seq = lengths.shape[0]
    earlier = jnp.arange(count_seq)[None, :] < jnp.arange(count_seq)[:, None]
    starts = jnp.sum(jnp.where(earlier, lengths[None, :], 0), axis=1)

    first = jnp.minimum(offsets[my_dp] + my_mp * half, seq_len - half)
    mine = jnp.stack(
        [
            lax.dynamic_slice_in_dim(embeds[0], first, half, axis=0),
            lax.dynamic_slice_in_dim(target_hidden[0], first, half, axis=0),
        ]
    )
    every = shifted(shifted(mine, "dp"), "mp")
    every = every.transpose(2, 0, 1, 3, 4).reshape(2, count_mp * count_dp * half, width)
    packed = jnp.arange(total_rows, dtype=jnp.int32)
    seq_all, slot_all, offset_all = locate(packed, starts, lengths, offsets)
    shift_mp = (my_mp - slot_all // half) % count_mp
    shift_dp = (my_dp - seq_all) % count_dp
    base = offset_all + (slot_all // half) * half
    lag = base - jnp.minimum(base, seq_len - half)
    within = jnp.minimum(slot_all % half + lag, half - 1)
    pick = (shift_mp * count_dp + shift_dp) * half + within
    embed_all = jnp.take(every[0], pick, axis=0)
    feature_all = jnp.take(every[1], pick, axis=0)
    flat = seq_all * seq_len + offset_all + slot_all
    ids = token_ids.reshape(-1)
    labels_all = jnp.sum(
        jnp.where(jnp.arange(ids.shape[0], dtype=jnp.int32)[None, :] == flat[:, None], ids, 0),
        axis=1,
    )

    partial_value = jnp.dot(embed_all, fc_embed, preferred_element_type=jnp.float32) + jnp.dot(
        feature_all, fc_feature, preferred_element_type=jnp.float32
    )
    target_square = jnp.sum(jnp.square(feature_all.astype(jnp.float32)), axis=1)
    piece = width // groups
    spare = pad_cols(-(-(total_rows + piece) // per_dev))
    gain_piece = lax.dynamic_slice_in_dim(draft_gain, (my_mp * count_dp + my_dp) * piece, piece)
    extra = jnp.pad(
        jnp.concatenate([target_square, gain_piece]),
        (0, per_dev * spare - total_rows - piece),
    ).reshape(per_dev, spare)
    send1 = jnp.concatenate(
        [
            partial_value.reshape(n_dev, per_dev, block),
            jnp.broadcast_to(extra[None], (n_dev,) + extra.shape),
        ],
        axis=2,
    )
    got1 = exchange(send1, ALL).reshape(count_sec, groups, per_dev, -1)
    hidden = (
        jnp.sum(got1[..., :block], axis=0).transpose(1, 0, 2).reshape(per_dev, groups * block)
    )
    extra_got = got1[..., block:].reshape(count_sec, groups, per_dev * spare)
    target_square = jnp.sum(extra_got[:, 0, :total_rows], axis=0)
    gain_full = extra_got[:, :, total_rows : total_rows + piece].reshape(full_width)
    target_scale = lax.rsqrt(target_square / D + eps_norm)
    target_norm = (feature_all.astype(jnp.float32) * target_scale[:, None] * target_gain).astype(
        jnp.bfloat16
    )
    draft_square = jnp.sum(hidden * hidden, axis=1)
    draft_scale = lax.rsqrt(draft_square / D + eps_norm)
    draft_norm = (hidden * draft_scale[:, None] * gain_full).astype(jnp.bfloat16)

    send2 = jnp.broadcast_to(
        draft_norm.reshape(per_dev, count_sec, 1, width).transpose(1, 2, 0, 3),
        (count_sec, groups, per_dev, width),
    ).reshape(n_dev, per_dev, width)
    draft_norm_all = exchange(send2, ALL).reshape(total_rows, width)

    target_logit = section_sum(contract_last(target_norm, head))
    draft_logit = section_sum(contract_last(draft_norm_all, head))
    column_zero = (my_mp * count_dp + my_dp) * vocab_tile
    is_label = (
        labels_all[:, None] - column_zero == jnp.arange(vocab_tile, dtype=jnp.int32)[None, :]
    )
    target_exp = jnp.exp(target_logit)
    sums = jnp.stack(
        [
            jnp.sum(target_exp, axis=1),
            jnp.sum(target_exp * draft_logit, axis=1),
            jnp.sum(jnp.exp(draft_logit), axis=1),
            jnp.sum(jnp.where(is_label, draft_logit, 0.0), axis=1),
        ]
    )
    sums = jnp.sum(
        exchange(jnp.broadcast_to(sums[None], (groups,) + sums.shape), ("mp", "dp")), axis=0
    )
    target_total, cross_total, draft_total, label_logit = sums[0], sums[1], sums[2], sums[3]
    draft_lse = jnp.log(draft_total)
    target_lse = jnp.log(target_total)
    row_loss = (
        draft_lse
        - (1.0 - label_mix) * cross_total / target_total
        - label_mix * label_logit
        + z_weight * draft_lse * draft_lse
    )
    loss = jnp.mean(row_loss)
    grad_tile = (
        (
            (1.0 + 2.0 * z_weight * draft_lse)[:, None] * jnp.exp(draft_logit - draft_lse[:, None])
            - (1.0 - label_mix) * jnp.exp(target_logit - target_lse[:, None])
            - label_mix * is_label.astype(jnp.float32)
        )
    ).astype(jnp.bfloat16)

    grad_part = jnp.dot(grad_tile, head, preferred_element_type=jnp.float32)
    by_mp = grad_part.reshape(count_sec, count_mp, count_dp, per_dev, width).transpose(1, 0, 2, 3, 4)
    reduced = lax.dynamic_index_in_dim(by_mp, my_mp, 0, keepdims=False)
    for k in range(1, count_mp):
        reduced = reduced + lax.ppermute(
            lax.dynamic_index_in_dim(by_mp, (my_mp + k) % count_mp, 0, keepdims=False),
            "mp",
            [(i, (i + k) % count_mp) for i in range(count_mp)],
        )
    send5 = reduced.reshape(count_sec * count_dp, per_dev, width)
    got5 = exchange(send5, ("section", "dp")).reshape(count_sec, count_dp, per_dev, width)
    draft_grad = jnp.sum(got5, axis=1).transpose(1, 0, 2).reshape(per_dev, full_width)
    upstream = draft_grad * gain_full
    inner_sum = jnp.sum(hidden * upstream, axis=1)
    hidden_grad = (
        draft_scale[:, None] * upstream - hidden * (draft_scale**3 * inner_sum / D)[:, None]
    ).astype(jnp.bfloat16)

    send6 = jnp.broadcast_to(
        hidden_grad.reshape(per_dev, 1, groups, block).transpose(1, 2, 0, 3),
        (count_sec, groups, per_dev, block),
    ).reshape(n_dev, per_dev, block)
    block_grad = exchange(send6, ALL).reshape(total_rows, block)
    grad_embed = contract_first(embed_all, block_grad)
    grad_feature = contract_first(feature_all, block_grad)
    return (loss, grad_embed, grad_feature)


def solution(mesh):
    return jax.shard_map(
        on_device,
        mesh=mesh,
        in_specs=(
            P("dp", None, "section"),
            P("dp", None, "section"),
            P(),
            P(),
            P(),
            P("section"),
            P("section"),
            P(("mp", "dp"), "section"),
            P("section", ("mp", "dp")),
            P("section", ("mp", "dp")),
        ),
        out_specs=(P(), P("section", ("mp", "dp")), P("section", ("mp", "dp"))),
        check_vma=False,
    )
```

```python
import jax
import jax.numpy as jnp
from jax import lax
from jax.sharding import PartitionSpec as P

D = 8192
R_OWN = 8


z_weight = 0.004
label_mix = 0.1
eps_norm = 1e-05

ALL = ("section", "mp", "dp")


def contract_last(operand, weights):
    return lax.dot_general(
        operand, weights, (((1,), (1,)), ((), ())), preferred_element_type=jnp.float32
    )


def contract_first(operand, weights):
    return lax.dot_general(
        operand, weights, (((0,), (0,)), ((), ())), preferred_element_type=jnp.float32
    )


def locate(packed, starts, lengths, offsets):
    rel = packed[:, None] - starts[None, :]
    inside = (rel >= 0) & (rel < lengths[None, :])
    seq = jnp.sum(jnp.where(inside, jnp.arange(starts.shape[0], dtype=jnp.int32)[None, :], 0), axis=1)
    slot = jnp.sum(jnp.where(inside, rel, 0), axis=1)
    offset = jnp.sum(jnp.where(inside, offsets[None, :], 0), axis=1)
    return seq, slot, offset


def exchange(send, axes):
    return lax.all_to_all(send, axes, split_axis=0, concat_axis=0, tiled=True)


def shifted(x, axis):
    count = lax.axis_size(axis)
    parts = [x] + [
        lax.ppermute(x, axis, [(i, (i + k) % count) for i in range(count)])
        for k in range(1, count)
    ]
    return jnp.stack(parts)


def section_sum(x):
    count = lax.axis_size("section")
    if count & (count - 1):
        mine = lax.axis_index("section")
        parts = jnp.stack(
            [x]
            + [
                lax.ppermute(x, "section", [(i, (i + k) % count) for i in range(count)])
                for k in range(1, count)
            ]
        )
        return jnp.sum(jnp.take(parts, (mine - jnp.arange(count)) % count, axis=0), axis=0)
    step = 1
    while step < count:
        x = x + lax.ppermute(x, "section", [(i, i ^ step) for i in range(count)])
        step *= 2
    return x


def pad_cols(count):
    return -(-count // 128) * 128


def on_device(
    target_hidden,
    embeds,
    token_ids,
    lengths,
    offsets,
    target_gain,
    draft_gain,
    head,
    fc_embed,
    fc_feature,
):
    count_dp = lax.axis_size("dp")
    count_mp = lax.axis_size("mp")
    count_sec = lax.axis_size("section")
    groups = count_mp * count_dp
    n_dev = count_sec * groups
    my_dp = lax.axis_index("dp")
    my_mp = lax.axis_index("mp")
    my_sec = lax.axis_index("section")
    me = (my_sec * count_mp + my_mp) * count_dp + my_dp
    width = target_hidden.shape[2]
    seq_len = target_hidden.shape[1]
    vocab_tile = head.shape[0]
    block = fc_embed.shape[1]
    full_width = width * count_sec
    total_rows = R_OWN * groups
    per_dev = total_rows // n_dev
    half = 2 * R_OWN
    count_seq = lengths.shape[0]
    earlier = jnp.arange(count_seq)[None, :] < jnp.arange(count_seq)[:, None]
    starts = jnp.sum(jnp.where(earlier, lengths[None, :], 0), axis=1)

    first = jnp.minimum(offsets[my_dp] + my_mp * half, seq_len - half)
    mine = jnp.stack(
        [
            lax.dynamic_slice_in_dim(embeds[0], first, half, axis=0),
            lax.dynamic_slice_in_dim(target_hidden[0], first, half, axis=0),
        ]
    )
    every = shifted(shifted(mine, "dp"), "mp")
    every = every.transpose(2, 0, 1, 3, 4).reshape(2, count_mp * count_dp * half, width)
    packed = jnp.arange(total_rows, dtype=jnp.int32)
    seq_all, slot_all, offset_all = locate(packed, starts, lengths, offsets)
    shift_mp = (my_mp - slot_all // half) % count_mp
    shift_dp = (my_dp - seq_all) % count_dp
    base = offset_all + (slot_all // half) * half
    lag = base - jnp.minimum(base, seq_len - half)
    within = jnp.minimum(slot_all % half + lag, half - 1)
    pick = (shift_mp * count_dp + shift_dp) * half + within
    embed_all = jnp.take(every[0], pick, axis=0)
    feature_all = jnp.take(every[1], pick, axis=0)
    flat = seq_all * seq_len + offset_all + slot_all
    ids = token_ids.reshape(-1)
    labels_all = jnp.sum(
        jnp.where(jnp.arange(ids.shape[0], dtype=jnp.int32)[None, :] == flat[:, None], ids, 0),
        axis=1,
    )

    partial_value = jnp.dot(embed_all, fc_embed, preferred_element_type=jnp.float32) + jnp.dot(
        feature_all, fc_feature, preferred_element_type=jnp.float32
    )
    target_square = section_sum(jnp.sum(jnp.square(feature_all.astype(jnp.float32)), axis=1))
    target_scale = lax.rsqrt(target_square / D + eps_norm)
    target_norm = (feature_all.astype(jnp.float32) * target_scale[:, None] * target_gain).astype(
        jnp.bfloat16
    )
    target_logit = section_sum(contract_last(target_norm, head))
    piece = width // groups
    spare = pad_cols(-(-piece // per_dev))
    gain_piece = lax.dynamic_slice_in_dim(draft_gain, (my_mp * count_dp + my_dp) * piece, piece)
    extra = jnp.pad(gain_piece, (0, per_dev * spare - piece)).reshape(per_dev, spare)
    send1 = jnp.concatenate(
        [
            partial_value.reshape(n_dev, per_dev, block),
            jnp.broadcast_to(extra[None], (n_dev,) + extra.shape),
        ],
        axis=2,
    )
    got1 = exchange(send1, ALL).reshape(count_sec, groups, per_dev, -1)
    hidden = (
        jnp.sum(got1[..., :block], axis=0).transpose(1, 0, 2).reshape(per_dev, groups * block)
    )
    extra_got = got1[..., block:].reshape(count_sec, groups, per_dev * spare)
    gain_full = extra_got[:, :, :piece].reshape(full_width)
    draft_square = jnp.sum(hidden * hidden, axis=1)
    draft_scale = lax.rsqrt(draft_square / D + eps_norm)
    draft_norm = (hidden * draft_scale[:, None] * gain_full).astype(jnp.bfloat16)

    send2 = jnp.broadcast_to(
        draft_norm.reshape(per_dev, count_sec, 1, width).transpose(1, 2, 0, 3),
        (count_sec, groups, per_dev, width),
    ).reshape(n_dev, per_dev, width)
    draft_norm_all = exchange(send2, ALL).reshape(total_rows, width)

    draft_logit = section_sum(contract_last(draft_norm_all, head))
    column_zero = (my_mp * count_dp + my_dp) * vocab_tile
    is_label = (
        labels_all[:, None] - column_zero == jnp.arange(vocab_tile, dtype=jnp.int32)[None, :]
    )
    target_exp = jnp.exp(target_logit)
    sums = jnp.stack(
        [
            jnp.sum(target_exp, axis=1),
            jnp.sum(target_exp * draft_logit, axis=1),
            jnp.sum(jnp.exp(draft_logit), axis=1),
            jnp.sum(jnp.where(is_label, draft_logit, 0.0), axis=1),
        ]
    )
    sums = jnp.sum(
        exchange(jnp.broadcast_to(sums[None], (groups,) + sums.shape), ("mp", "dp")), axis=0
    )
    target_total, cross_total, draft_total, label_logit = sums[0], sums[1], sums[2], sums[3]
    draft_lse = jnp.log(draft_total)
    target_lse = jnp.log(target_total)
    row_loss = (
        draft_lse
        - (1.0 - label_mix) * cross_total / target_total
        - label_mix * label_logit
        + z_weight * draft_lse * draft_lse
    )
    loss = jnp.mean(row_loss)
    grad_tile = (
        (
            (1.0 + 2.0 * z_weight * draft_lse)[:, None] * jnp.exp(draft_logit - draft_lse[:, None])
            - (1.0 - label_mix) * jnp.exp(target_logit - target_lse[:, None])
            - label_mix * is_label.astype(jnp.float32)
        )
    ).astype(jnp.bfloat16)

    grad_part = jnp.dot(grad_tile, head, preferred_element_type=jnp.float32)
    by_mp = grad_part.reshape(count_sec, count_mp, count_dp, per_dev, width).transpose(1, 0, 2, 3, 4)
    reduced = lax.dynamic_index_in_dim(by_mp, my_mp, 0, keepdims=False)
    for k in range(1, count_mp):
        reduced = reduced + lax.ppermute(
            lax.dynamic_index_in_dim(by_mp, (my_mp + k) % count_mp, 0, keepdims=False),
            "mp",
            [(i, (i + k) % count_mp) for i in range(count_mp)],
        )
    send5 = reduced.reshape(count_sec * count_dp, per_dev, width)
    got5 = exchange(send5, ("section", "dp")).reshape(count_sec, count_dp, per_dev, width)
    draft_grad = jnp.sum(got5, axis=1).transpose(1, 0, 2).reshape(per_dev, full_width)
    upstream = draft_grad * gain_full
    inner_sum = jnp.sum(hidden * upstream, axis=1)
    hidden_grad = (
        draft_scale[:, None] * upstream - hidden * (draft_scale**3 * inner_sum / D)[:, None]
    ).astype(jnp.bfloat16)

    send6 = jnp.broadcast_to(
        hidden_grad.reshape(per_dev, 1, groups, block).transpose(1, 2, 0, 3),
        (count_sec, groups, per_dev, block),
    ).reshape(n_dev, per_dev, block)
    block_grad = exchange(send6, ALL).reshape(total_rows, block)
    grad_embed = contract_first(embed_all, block_grad)
    grad_feature = contract_first(feature_all, block_grad)
    return (loss, grad_embed, grad_feature)


def solution(mesh):
    return jax.shard_map(
        on_device,
        mesh=mesh,
        in_specs=(
            P("dp", None, "section"),
            P("dp", None, "section"),
            P(),
            P(),
            P(),
            P("section"),
            P("section"),
            P(("mp", "dp"), "section"),
            P("section", ("mp", "dp")),
            P("section", ("mp", "dp")),
        ),
        out_specs=(P(), P("section", ("mp", "dp")), P("section", ("mp", "dp"))),
        check_vma=False,
    )
```

```python
import jax
import jax.numpy as jnp
from jax import lax
from jax.sharding import PartitionSpec as P

D = 8192
R_OWN = 8


z_weight = 0.004
label_mix = 0.1
eps_norm = 1e-05

ALL = ("section", "mp", "dp")


def contract_last(operand, weights):
    return lax.dot_general(
        operand, weights, (((1,), (1,)), ((), ())), preferred_element_type=jnp.float32
    )


def contract_first(operand, weights):
    return lax.dot_general(
        operand, weights, (((0,), (0,)), ((), ())), preferred_element_type=jnp.float32
    )


def locate(packed, starts, lengths, offsets):
    rel = packed[:, None] - starts[None, :]
    inside = (rel >= 0) & (rel < lengths[None, :])
    seq = jnp.sum(jnp.where(inside, jnp.arange(starts.shape[0], dtype=jnp.int32)[None, :], 0), axis=1)
    slot = jnp.sum(jnp.where(inside, rel, 0), axis=1)
    offset = jnp.sum(jnp.where(inside, offsets[None, :], 0), axis=1)
    return seq, slot, offset


def exchange(send, axes):
    return lax.all_to_all(send, axes, split_axis=0, concat_axis=0, tiled=True)


def shifted(x, axis):
    count = lax.axis_size(axis)
    parts = [x] + [
        lax.ppermute(x, axis, [(i, (i + k) % count) for i in range(count)])
        for k in range(1, count)
    ]
    return jnp.stack(parts)


def section_sum(x):
    count = lax.axis_size("section")
    if count & (count - 1):
        mine = lax.axis_index("section")
        parts = jnp.stack(
            [x]
            + [
                lax.ppermute(x, "section", [(i, (i + k) % count) for i in range(count)])
                for k in range(1, count)
            ]
        )
        return jnp.sum(jnp.take(parts, (mine - jnp.arange(count)) % count, axis=0), axis=0)
    step = 1
    while step < count:
        x = x + lax.ppermute(x, "section", [(i, i ^ step) for i in range(count)])
        step *= 2
    return x


def pad_cols(count):
    return -(-count // 128) * 128


def on_device(
    target_hidden,
    embeds,
    token_ids,
    lengths,
    offsets,
    target_gain,
    draft_gain,
    head,
    fc_embed,
    fc_feature,
):
    count_dp = lax.axis_size("dp")
    count_mp = lax.axis_size("mp")
    count_sec = lax.axis_size("section")
    groups = count_mp * count_dp
    n_dev = count_sec * groups
    my_dp = lax.axis_index("dp")
    my_mp = lax.axis_index("mp")
    my_sec = lax.axis_index("section")
    me = (my_sec * count_mp + my_mp) * count_dp + my_dp
    width = target_hidden.shape[2]
    seq_len = target_hidden.shape[1]
    vocab_tile = head.shape[0]
    block = fc_embed.shape[1]
    full_width = width * count_sec
    total_rows = R_OWN * groups
    per_dev = total_rows // n_dev
    half = 2 * R_OWN
    count_seq = lengths.shape[0]
    earlier = jnp.arange(count_seq)[None, :] < jnp.arange(count_seq)[:, None]
    starts = jnp.sum(jnp.where(earlier, lengths[None, :], 0), axis=1)

    first = jnp.minimum(offsets[my_dp] + my_mp * half, seq_len - half)
    mine = jnp.stack(
        [
            lax.dynamic_slice_in_dim(embeds[0], first, half, axis=0),
            lax.dynamic_slice_in_dim(target_hidden[0], first, half, axis=0),
        ]
    )
    every = shifted(shifted(mine, "dp"), "mp")
    every = every.transpose(2, 0, 1, 3, 4).reshape(2, count_mp * count_dp * half, width)
    packed = jnp.arange(total_rows, dtype=jnp.int32)
    seq_all, slot_all, offset_all = locate(packed, starts, lengths, offsets)
    shift_mp = (my_mp - slot_all // half) % count_mp
    shift_dp = (my_dp - seq_all) % count_dp
    base = offset_all + (slot_all // half) * half
    lag = base - jnp.minimum(base, seq_len - half)
    within = jnp.minimum(slot_all % half + lag, half - 1)
    pick = (shift_mp * count_dp + shift_dp) * half + within
    embed_all = jnp.take(every[0], pick, axis=0)
    feature_all = jnp.take(every[1], pick, axis=0)
    flat = seq_all * seq_len + offset_all + slot_all
    ids = token_ids.reshape(-1)
    labels_all = jnp.sum(
        jnp.where(jnp.arange(ids.shape[0], dtype=jnp.int32)[None, :] == flat[:, None], ids, 0),
        axis=1,
    )

    partial_value = jnp.dot(embed_all, fc_embed, preferred_element_type=jnp.float32) + jnp.dot(
        feature_all, fc_feature, preferred_element_type=jnp.float32
    )
    target_square = section_sum(jnp.sum(jnp.square(feature_all.astype(jnp.float32)), axis=1))
    target_scale = lax.rsqrt(target_square / D + eps_norm)
    target_norm = (feature_all.astype(jnp.float32) * target_scale[:, None] * target_gain).astype(
        jnp.bfloat16
    )
    target_part = contract_last(target_norm, head)
    piece = width // groups
    spare = pad_cols(-(-piece // per_dev))
    gain_piece = lax.dynamic_slice_in_dim(draft_gain, (my_mp * count_dp + my_dp) * piece, piece)
    extra = jnp.pad(gain_piece, (0, per_dev * spare - piece)).reshape(per_dev, spare)
    send1 = jnp.concatenate(
        [
            partial_value.reshape(n_dev, per_dev, block),
            jnp.broadcast_to(extra[None], (n_dev,) + extra.shape),
        ],
        axis=2,
    )
    got1, target_logit = lax.optimization_barrier((exchange(send1, ALL), section_sum(target_part)))
    got1 = got1.reshape(count_sec, groups, per_dev, -1)
    hidden = (
        jnp.sum(got1[..., :block], axis=0).transpose(1, 0, 2).reshape(per_dev, groups * block)
    )
    extra_got = got1[..., block:].reshape(count_sec, groups, per_dev * spare)
    gain_full = extra_got[:, :, :piece].reshape(full_width)
    draft_square = jnp.sum(hidden * hidden, axis=1)
    draft_scale = lax.rsqrt(draft_square / D + eps_norm)
    draft_norm = (hidden * draft_scale[:, None] * gain_full).astype(jnp.bfloat16)

    send2 = jnp.broadcast_to(
        draft_norm.reshape(per_dev, count_sec, 1, width).transpose(1, 2, 0, 3),
        (count_sec, groups, per_dev, width),
    ).reshape(n_dev, per_dev, width)
    draft_norm_all = exchange(send2, ALL).reshape(total_rows, width)

    draft_logit = section_sum(contract_last(draft_norm_all, head))
    column_zero = (my_mp * count_dp + my_dp) * vocab_tile
    is_label = (
        labels_all[:, None] - column_zero == jnp.arange(vocab_tile, dtype=jnp.int32)[None, :]
    )
    target_exp = jnp.exp(target_logit)
    sums = jnp.stack(
        [
            jnp.sum(target_exp, axis=1),
            jnp.sum(target_exp * draft_logit, axis=1),
            jnp.sum(jnp.exp(draft_logit), axis=1),
            jnp.sum(jnp.where(is_label, draft_logit, 0.0), axis=1),
        ]
    )
    sums = jnp.sum(
        exchange(jnp.broadcast_to(sums[None], (groups,) + sums.shape), ("mp", "dp")), axis=0
    )
    target_total, cross_total, draft_total, label_logit = sums[0], sums[1], sums[2], sums[3]
    draft_lse = jnp.log(draft_total)
    target_lse = jnp.log(target_total)
    row_loss = (
        draft_lse
        - (1.0 - label_mix) * cross_total / target_total
        - label_mix * label_logit
        + z_weight * draft_lse * draft_lse
    )
    loss = jnp.mean(row_loss)
    grad_tile = (
        (
            (1.0 + 2.0 * z_weight * draft_lse)[:, None] * jnp.exp(draft_logit - draft_lse[:, None])
            - (1.0 - label_mix) * jnp.exp(target_logit - target_lse[:, None])
            - label_mix * is_label.astype(jnp.float32)
        )
    ).astype(jnp.bfloat16)

    grad_part = jnp.dot(grad_tile, head, preferred_element_type=jnp.float32)
    by_mp = grad_part.reshape(count_sec, count_mp, count_dp, per_dev, width).transpose(1, 0, 2, 3, 4)
    reduced = lax.dynamic_index_in_dim(by_mp, my_mp, 0, keepdims=False)
    for k in range(1, count_mp):
        reduced = reduced + lax.ppermute(
            lax.dynamic_index_in_dim(by_mp, (my_mp + k) % count_mp, 0, keepdims=False),
            "mp",
            [(i, (i + k) % count_mp) for i in range(count_mp)],
        )
    send5 = reduced.reshape(count_sec * count_dp, per_dev, width)
    got5 = exchange(send5, ("section", "dp")).reshape(count_sec, count_dp, per_dev, width)
    draft_grad = jnp.sum(got5, axis=1).transpose(1, 0, 2).reshape(per_dev, full_width)
    upstream = draft_grad * gain_full
    inner_sum = jnp.sum(hidden * upstream, axis=1)
    hidden_grad = (
        draft_scale[:, None] * upstream - hidden * (draft_scale**3 * inner_sum / D)[:, None]
    ).astype(jnp.bfloat16)

    send6 = jnp.broadcast_to(
        hidden_grad.reshape(per_dev, 1, groups, block).transpose(1, 2, 0, 3),
        (count_sec, groups, per_dev, block),
    ).reshape(n_dev, per_dev, block)
    block_grad = exchange(send6, ALL).reshape(total_rows, block)
    grad_embed = contract_first(embed_all, block_grad)
    grad_feature = contract_first(feature_all, block_grad)
    return (loss, grad_embed, grad_feature)


def solution(mesh):
    return jax.shard_map(
        on_device,
        mesh=mesh,
        in_specs=(
            P("dp", None, "section"),
            P("dp", None, "section"),
            P(),
            P(),
            P(),
            P("section"),
            P("section"),
            P(("mp", "dp"), "section"),
            P("section", ("mp", "dp")),
            P("section", ("mp", "dp")),
        ),
        out_specs=(P(), P("section", ("mp", "dp")), P("section", ("mp", "dp"))),
        check_vma=False,
    )
```

```python
import jax
import jax.numpy as jnp
from jax import lax
from jax.sharding import PartitionSpec as P

D = 8192
R_OWN = 8


z_weight = 0.004
label_mix = 0.1
eps_norm = 1e-05

ALL = ("section", "mp", "dp")


def contract_last(operand, weights):
    return lax.dot_general(
        operand, weights, (((1,), (1,)), ((), ())), preferred_element_type=jnp.float32
    )


def contract_first(operand, weights):
    return lax.dot_general(
        operand, weights, (((0,), (0,)), ((), ())), preferred_element_type=jnp.float32
    )


def locate(packed, starts, lengths, offsets):
    rel = packed[:, None] - starts[None, :]
    inside = (rel >= 0) & (rel < lengths[None, :])
    seq = jnp.sum(jnp.where(inside, jnp.arange(starts.shape[0], dtype=jnp.int32)[None, :], 0), axis=1)
    slot = jnp.sum(jnp.where(inside, rel, 0), axis=1)
    offset = jnp.sum(jnp.where(inside, offsets[None, :], 0), axis=1)
    return seq, slot, offset


def exchange(send, axes):
    return lax.all_to_all(send, axes, split_axis=0, concat_axis=0, tiled=True)


def shifted(x, axis):
    count = lax.axis_size(axis)
    parts = [x] + [
        lax.ppermute(x, axis, [(i, (i + k) % count) for i in range(count)])
        for k in range(1, count)
    ]
    return jnp.stack(parts)


def section_sum(x):
    count = lax.axis_size("section")
    if count & (count - 1):
        mine = lax.axis_index("section")
        parts = jnp.stack(
            [x]
            + [
                lax.ppermute(x, "section", [(i, (i + k) % count) for i in range(count)])
                for k in range(1, count)
            ]
        )
        return jnp.sum(jnp.take(parts, (mine - jnp.arange(count)) % count, axis=0), axis=0)
    count_mp = lax.axis_size("mp")
    steps = [1 << b for b in range(count.bit_length() - 1)]
    for level in range(len(steps)):
        pairs = []
        for i in range(count):
            for m in range(count_mp):
                step = steps[level] if m % 2 == 0 else steps[len(steps) - 1 - level]
                pairs.append((i * count_mp + m, (i ^ step) * count_mp + m))
        x = x + lax.ppermute(x, ("section", "mp"), pairs)
    return x


def pad_cols(count):
    return -(-count // 128) * 128


def on_device(
    target_hidden,
    embeds,
    token_ids,
    lengths,
    offsets,
    target_gain,
    draft_gain,
    head,
    fc_embed,
    fc_feature,
):
    count_dp = lax.axis_size("dp")
    count_mp = lax.axis_size("mp")
    count_sec = lax.axis_size("section")
    groups = count_mp * count_dp
    n_dev = count_sec * groups
    my_dp = lax.axis_index("dp")
    my_mp = lax.axis_index("mp")
    my_sec = lax.axis_index("section")
    me = (my_sec * count_mp + my_mp) * count_dp + my_dp
    width = target_hidden.shape[2]
    seq_len = target_hidden.shape[1]
    vocab_tile = head.shape[0]
    block = fc_embed.shape[1]
    full_width = width * count_sec
    total_rows = R_OWN * groups
    per_dev = total_rows // n_dev
    half = 2 * R_OWN
    count_seq = lengths.shape[0]
    earlier = jnp.arange(count_seq)[None, :] < jnp.arange(count_seq)[:, None]
    starts = jnp.sum(jnp.where(earlier, lengths[None, :], 0), axis=1)

    first = jnp.minimum(offsets[my_dp] + my_mp * half, seq_len - half)
    mine = jnp.stack(
        [
            lax.dynamic_slice_in_dim(embeds[0], first, half, axis=0),
            lax.dynamic_slice_in_dim(target_hidden[0], first, half, axis=0),
        ]
    )
    every = shifted(shifted(mine, "dp"), "mp")
    every = every.transpose(2, 0, 1, 3, 4).reshape(2, count_mp * count_dp * half, width)
    packed = jnp.arange(total_rows, dtype=jnp.int32)
    seq_all, slot_all, offset_all = locate(packed, starts, lengths, offsets)
    shift_mp = (my_mp - slot_all // half) % count_mp
    shift_dp = (my_dp - seq_all) % count_dp
    base = offset_all + (slot_all // half) * half
    lag = base - jnp.minimum(base, seq_len - half)
    within = jnp.minimum(slot_all % half + lag, half - 1)
    pick = (shift_mp * count_dp + shift_dp) * half + within
    embed_all = jnp.take(every[0], pick, axis=0)
    feature_all = jnp.take(every[1], pick, axis=0)
    flat = seq_all * seq_len + offset_all + slot_all
    ids = token_ids.reshape(-1)
    labels_all = jnp.sum(
        jnp.where(jnp.arange(ids.shape[0], dtype=jnp.int32)[None, :] == flat[:, None], ids, 0),
        axis=1,
    )

    partial_value = jnp.dot(embed_all, fc_embed, preferred_element_type=jnp.float32) + jnp.dot(
        feature_all, fc_feature, preferred_element_type=jnp.float32
    )
    target_square = section_sum(jnp.sum(jnp.square(feature_all.astype(jnp.float32)), axis=1))
    target_scale = lax.rsqrt(target_square / D + eps_norm)
    target_norm = (feature_all.astype(jnp.float32) * target_scale[:, None] * target_gain).astype(
        jnp.bfloat16
    )
    target_logit = section_sum(contract_last(target_norm, head))
    piece = width // groups
    spare = pad_cols(-(-piece // per_dev))
    gain_piece = lax.dynamic_slice_in_dim(draft_gain, (my_mp * count_dp + my_dp) * piece, piece)
    extra = jnp.pad(gain_piece, (0, per_dev * spare - piece)).reshape(per_dev, spare)
    send1 = jnp.concatenate(
        [
            partial_value.reshape(n_dev, per_dev, block),
            jnp.broadcast_to(extra[None], (n_dev,) + extra.shape),
        ],
        axis=2,
    )
    got1 = exchange(send1, ALL).reshape(count_sec, groups, per_dev, -1)
    hidden = (
        jnp.sum(got1[..., :block], axis=0).transpose(1, 0, 2).reshape(per_dev, groups * block)
    )
    extra_got = got1[..., block:].reshape(count_sec, groups, per_dev * spare)
    gain_full = extra_got[:, :, :piece].reshape(full_width)
    draft_square = jnp.sum(hidden * hidden, axis=1)
    draft_scale = lax.rsqrt(draft_square / D + eps_norm)
    draft_norm = (hidden * draft_scale[:, None] * gain_full).astype(jnp.bfloat16)

    send2 = jnp.broadcast_to(
        draft_norm.reshape(per_dev, count_sec, 1, width).transpose(1, 2, 0, 3),
        (count_sec, groups, per_dev, width),
    ).reshape(n_dev, per_dev, width)
    draft_norm_all = exchange(send2, ALL).reshape(total_rows, width)

    draft_logit = section_sum(contract_last(draft_norm_all, head))
    column_zero = (my_mp * count_dp + my_dp) * vocab_tile
    is_label = (
        labels_all[:, None] - column_zero == jnp.arange(vocab_tile, dtype=jnp.int32)[None, :]
    )
    target_exp = jnp.exp(target_logit)
    sums = jnp.stack(
        [
            jnp.sum(target_exp, axis=1),
            jnp.sum(target_exp * draft_logit, axis=1),
            jnp.sum(jnp.exp(draft_logit), axis=1),
            jnp.sum(jnp.where(is_label, draft_logit, 0.0), axis=1),
        ]
    )
    sums = jnp.sum(
        exchange(jnp.broadcast_to(sums[None], (groups,) + sums.shape), ("mp", "dp")), axis=0
    )
    target_total, cross_total, draft_total, label_logit = sums[0], sums[1], sums[2], sums[3]
    draft_lse = jnp.log(draft_total)
    target_lse = jnp.log(target_total)
    row_loss = (
        draft_lse
        - (1.0 - label_mix) * cross_total / target_total
        - label_mix * label_logit
        + z_weight * draft_lse * draft_lse
    )
    loss = jnp.mean(row_loss)
    grad_tile = (
        (
            (1.0 + 2.0 * z_weight * draft_lse)[:, None] * jnp.exp(draft_logit - draft_lse[:, None])
            - (1.0 - label_mix) * jnp.exp(target_logit - target_lse[:, None])
            - label_mix * is_label.astype(jnp.float32)
        )
    ).astype(jnp.bfloat16)

    grad_part = jnp.dot(grad_tile, head, preferred_element_type=jnp.float32)
    by_mp = grad_part.reshape(count_sec, count_mp, count_dp, per_dev, width).transpose(1, 0, 2, 3, 4)
    reduced = lax.dynamic_index_in_dim(by_mp, my_mp, 0, keepdims=False)
    for k in range(1, count_mp):
        reduced = reduced + lax.ppermute(
            lax.dynamic_index_in_dim(by_mp, (my_mp + k) % count_mp, 0, keepdims=False),
            "mp",
            [(i, (i + k) % count_mp) for i in range(count_mp)],
        )
    send5 = reduced.reshape(count_sec * count_dp, per_dev, width)
    got5 = exchange(send5, ("section", "dp")).reshape(count_sec, count_dp, per_dev, width)
    draft_grad = jnp.sum(got5, axis=1).transpose(1, 0, 2).reshape(per_dev, full_width)
    upstream = draft_grad * gain_full
    inner_sum = jnp.sum(hidden * upstream, axis=1)
    hidden_grad = (
        draft_scale[:, None] * upstream - hidden * (draft_scale**3 * inner_sum / D)[:, None]
    ).astype(jnp.bfloat16)

    send6 = jnp.broadcast_to(
        hidden_grad.reshape(per_dev, 1, groups, block).transpose(1, 2, 0, 3),
        (count_sec, groups, per_dev, block),
    ).reshape(n_dev, per_dev, block)
    block_grad = exchange(send6, ALL).reshape(total_rows, block)
    grad_embed = contract_first(embed_all, block_grad)
    grad_feature = contract_first(feature_all, block_grad)
    return (loss, grad_embed, grad_feature)


def solution(mesh):
    return jax.shard_map(
        on_device,
        mesh=mesh,
        in_specs=(
            P("dp", None, "section"),
            P("dp", None, "section"),
            P(),
            P(),
            P(),
            P("section"),
            P("section"),
            P(("mp", "dp"), "section"),
            P("section", ("mp", "dp")),
            P("section", ("mp", "dp")),
        ),
        out_specs=(P(), P("section", ("mp", "dp")), P("section", ("mp", "dp"))),
        check_vma=False,
    )
```

```python
import jax
import jax.numpy as jnp
from jax import lax
from jax.sharding import PartitionSpec as P

D = 8192
R_OWN = 8


z_weight = 0.004
label_mix = 0.1
eps_norm = 1e-05

ALL = ("section", "mp", "dp")


def contract_last(operand, weights):
    return lax.dot_general(
        operand, weights, (((1,), (1,)), ((), ())), preferred_element_type=jnp.float32
    )


def contract_first(operand, weights):
    return lax.dot_general(
        operand, weights, (((0,), (0,)), ((), ())), preferred_element_type=jnp.float32
    )


def locate(packed, starts, lengths, offsets):
    rel = packed[:, None] - starts[None, :]
    inside = (rel >= 0) & (rel < lengths[None, :])
    seq = jnp.sum(jnp.where(inside, jnp.arange(starts.shape[0], dtype=jnp.int32)[None, :], 0), axis=1)
    slot = jnp.sum(jnp.where(inside, rel, 0), axis=1)
    offset = jnp.sum(jnp.where(inside, offsets[None, :], 0), axis=1)
    return seq, slot, offset


def exchange(send, axes):
    return lax.all_to_all(send, axes, split_axis=0, concat_axis=0, tiled=True)


def shifted(x, axis):
    count = lax.axis_size(axis)
    parts = [x] + [
        lax.ppermute(x, axis, [(i, (i + k) % count) for i in range(count)])
        for k in range(1, count)
    ]
    return jnp.stack(parts)


def section_sum(x):
    count = lax.axis_size("section")
    if count & (count - 1):
        mine = lax.axis_index("section")
        parts = jnp.stack(
            [x]
            + [
                lax.ppermute(x, "section", [(i, (i + k) % count) for i in range(count)])
                for k in range(1, count)
            ]
        )
        return jnp.sum(jnp.take(parts, (mine - jnp.arange(count)) % count, axis=0), axis=0)
    count_mp = lax.axis_size("mp")
    steps = [1 << b for b in range(count.bit_length() - 1)]
    for level in range(len(steps)):
        pairs = []
        for i in range(count):
            for m in range(count_mp):
                step = steps[level] if m % 2 == 0 else steps[len(steps) - 1 - level]
                pairs.append((i * count_mp + m, (i ^ step) * count_mp + m))
        x = x + lax.ppermute(x, ("section", "mp"), pairs)
    return x


def pad_cols(count):
    return -(-count // 128) * 128


def on_device(
    target_hidden,
    embeds,
    token_ids,
    lengths,
    offsets,
    target_gain,
    draft_gain,
    head,
    fc_embed,
    fc_feature,
):
    count_dp = lax.axis_size("dp")
    count_mp = lax.axis_size("mp")
    count_sec = lax.axis_size("section")
    groups = count_mp * count_dp
    n_dev = count_sec * groups
    my_dp = lax.axis_index("dp")
    my_mp = lax.axis_index("mp")
    my_sec = lax.axis_index("section")
    me = (my_sec * count_mp + my_mp) * count_dp + my_dp
    width = target_hidden.shape[2]
    seq_len = target_hidden.shape[1]
    vocab_tile = head.shape[0]
    block = fc_embed.shape[1]
    full_width = width * count_sec
    total_rows = R_OWN * groups
    per_dev = total_rows // n_dev
    half = 2 * R_OWN
    count_seq = lengths.shape[0]
    earlier = jnp.arange(count_seq)[None, :] < jnp.arange(count_seq)[:, None]
    starts = jnp.sum(jnp.where(earlier, lengths[None, :], 0), axis=1)

    first = jnp.minimum(offsets[my_dp] + my_mp * half, seq_len - half)
    mine = jnp.stack(
        [
            lax.dynamic_slice_in_dim(embeds[0], first, half, axis=0),
            lax.dynamic_slice_in_dim(target_hidden[0], first, half, axis=0),
        ]
    )
    every = shifted(shifted(mine, "dp"), "mp")
    every = every.transpose(2, 0, 1, 3, 4).reshape(2, count_mp * count_dp * half, width)
    packed = jnp.arange(total_rows, dtype=jnp.int32)
    seq_all, slot_all, offset_all = locate(packed, starts, lengths, offsets)
    shift_mp = (my_mp - slot_all // half) % count_mp
    shift_dp = (my_dp - seq_all) % count_dp
    base = offset_all + (slot_all // half) * half
    lag = base - jnp.minimum(base, seq_len - half)
    within = jnp.minimum(slot_all % half + lag, half - 1)
    pick = (shift_mp * count_dp + shift_dp) * half + within
    embed_all = jnp.take(every[0], pick, axis=0)
    feature_all = jnp.take(every[1], pick, axis=0)
    flat = seq_all * seq_len + offset_all + slot_all
    ids = token_ids.reshape(-1)
    labels_all = jnp.sum(
        jnp.where(jnp.arange(ids.shape[0], dtype=jnp.int32)[None, :] == flat[:, None], ids, 0),
        axis=1,
    )

    partial_value = jnp.dot(embed_all, fc_embed, preferred_element_type=jnp.float32) + jnp.dot(
        feature_all, fc_feature, preferred_element_type=jnp.float32
    )
    target_square = section_sum(jnp.sum(jnp.square(feature_all.astype(jnp.float32)), axis=1))
    target_scale = lax.rsqrt(target_square / D + eps_norm)
    target_norm = (feature_all.astype(jnp.float32) * target_scale[:, None] * target_gain).astype(
        jnp.bfloat16
    )
    target_part = contract_last(target_norm, head)
    piece = width // groups
    spare = pad_cols(-(-piece // per_dev))
    gain_piece = lax.dynamic_slice_in_dim(draft_gain, (my_mp * count_dp + my_dp) * piece, piece)
    extra = jnp.pad(gain_piece, (0, per_dev * spare - piece)).reshape(per_dev, spare)
    send1 = jnp.concatenate(
        [
            partial_value.reshape(n_dev, per_dev, block),
            jnp.broadcast_to(extra[None], (n_dev,) + extra.shape),
        ],
        axis=2,
    )
    got1, target_part = lax.optimization_barrier((exchange(send1, ALL), target_part))
    target_logit = section_sum(target_part)
    got1 = got1.reshape(count_sec, groups, per_dev, -1)
    hidden = (
        jnp.sum(got1[..., :block], axis=0).transpose(1, 0, 2).reshape(per_dev, groups * block)
    )
    extra_got = got1[..., block:].reshape(count_sec, groups, per_dev * spare)
    gain_full = extra_got[:, :, :piece].reshape(full_width)
    draft_square = jnp.sum(hidden * hidden, axis=1)
    draft_scale = lax.rsqrt(draft_square / D + eps_norm)
    draft_norm = (hidden * draft_scale[:, None] * gain_full).astype(jnp.bfloat16)

    send2 = jnp.broadcast_to(
        draft_norm.reshape(per_dev, count_sec, 1, width).transpose(1, 2, 0, 3),
        (count_sec, groups, per_dev, width),
    ).reshape(n_dev, per_dev, width)
    draft_norm_all = exchange(send2, ALL).reshape(total_rows, width)

    draft_logit = section_sum(contract_last(draft_norm_all, head))
    column_zero = (my_mp * count_dp + my_dp) * vocab_tile
    is_label = (
        labels_all[:, None] - column_zero == jnp.arange(vocab_tile, dtype=jnp.int32)[None, :]
    )
    target_exp = jnp.exp(target_logit)
    sums = jnp.stack(
        [
            jnp.sum(target_exp, axis=1),
            jnp.sum(target_exp * draft_logit, axis=1),
            jnp.sum(jnp.exp(draft_logit), axis=1),
            jnp.sum(jnp.where(is_label, draft_logit, 0.0), axis=1),
        ]
    )
    sums = jnp.sum(
        exchange(jnp.broadcast_to(sums[None], (groups,) + sums.shape), ("mp", "dp")), axis=0
    )
    target_total, cross_total, draft_total, label_logit = sums[0], sums[1], sums[2], sums[3]
    draft_lse = jnp.log(draft_total)
    target_lse = jnp.log(target_total)
    row_loss = (
        draft_lse
        - (1.0 - label_mix) * cross_total / target_total
        - label_mix * label_logit
        + z_weight * draft_lse * draft_lse
    )
    loss = jnp.mean(row_loss)
    grad_tile = (
        (
            (1.0 + 2.0 * z_weight * draft_lse)[:, None] * jnp.exp(draft_logit - draft_lse[:, None])
            - (1.0 - label_mix) * jnp.exp(target_logit - target_lse[:, None])
            - label_mix * is_label.astype(jnp.float32)
        )
    ).astype(jnp.bfloat16)

    grad_part = jnp.dot(grad_tile, head, preferred_element_type=jnp.float32)
    by_mp = grad_part.reshape(count_sec, count_mp, count_dp, per_dev, width).transpose(1, 0, 2, 3, 4)
    reduced = lax.dynamic_index_in_dim(by_mp, my_mp, 0, keepdims=False)
    for k in range(1, count_mp):
        reduced = reduced + lax.ppermute(
            lax.dynamic_index_in_dim(by_mp, (my_mp + k) % count_mp, 0, keepdims=False),
            "mp",
            [(i, (i + k) % count_mp) for i in range(count_mp)],
        )
    send5 = reduced.reshape(count_sec * count_dp, per_dev, width)
    got5 = exchange(send5, ("section", "dp")).reshape(count_sec, count_dp, per_dev, width)
    draft_grad = jnp.sum(got5, axis=1).transpose(1, 0, 2).reshape(per_dev, full_width)
    upstream = draft_grad * gain_full
    inner_sum = jnp.sum(hidden * upstream, axis=1)
    hidden_grad = (
        draft_scale[:, None] * upstream - hidden * (draft_scale**3 * inner_sum / D)[:, None]
    ).astype(jnp.bfloat16)

    send6 = jnp.broadcast_to(
        hidden_grad.reshape(per_dev, 1, groups, block).transpose(1, 2, 0, 3),
        (count_sec, groups, per_dev, block),
    ).reshape(n_dev, per_dev, block)
    block_grad = exchange(send6, ALL).reshape(total_rows, block)
    grad_embed = contract_first(embed_all, block_grad)
    grad_feature = contract_first(feature_all, block_grad)
    return (loss, grad_embed, grad_feature)


def solution(mesh):
    return jax.shard_map(
        on_device,
        mesh=mesh,
        in_specs=(
            P("dp", None, "section"),
            P("dp", None, "section"),
            P(),
            P(),
            P(),
            P("section"),
            P("section"),
            P(("mp", "dp"), "section"),
            P("section", ("mp", "dp")),
            P("section", ("mp", "dp")),
        ),
        out_specs=(P(), P("section", ("mp", "dp")), P("section", ("mp", "dp"))),
        check_vma=False,
    )
```

```python
import jax
import jax.numpy as jnp
from jax import lax
from jax.sharding import PartitionSpec as P

D = 8192
R_OWN = 8


z_weight = 0.004
label_mix = 0.1
eps_norm = 1e-05

ALL = ("section", "mp", "dp")


def contract_last(operand, weights):
    return lax.dot_general(
        operand, weights, (((1,), (1,)), ((), ())), preferred_element_type=jnp.float32
    )


def contract_first(operand, weights):
    return lax.dot_general(
        operand, weights, (((0,), (0,)), ((), ())), preferred_element_type=jnp.float32
    )


def locate(packed, starts, lengths, offsets):
    rel = packed[:, None] - starts[None, :]
    inside = (rel >= 0) & (rel < lengths[None, :])
    seq = jnp.sum(jnp.where(inside, jnp.arange(starts.shape[0], dtype=jnp.int32)[None, :], 0), axis=1)
    slot = jnp.sum(jnp.where(inside, rel, 0), axis=1)
    offset = jnp.sum(jnp.where(inside, offsets[None, :], 0), axis=1)
    return seq, slot, offset


def exchange(send, axes):
    return lax.all_to_all(send, axes, split_axis=0, concat_axis=0, tiled=True)


def shifted(x, axis):
    count = lax.axis_size(axis)
    parts = [x] + [
        lax.ppermute(x, axis, [(i, (i + k) % count) for i in range(count)])
        for k in range(1, count)
    ]
    return jnp.stack(parts)


def section_sum(x):
    count = lax.axis_size("section")
    if count & (count - 1):
        mine = lax.axis_index("section")
        parts = jnp.stack(
            [x]
            + [
                lax.ppermute(x, "section", [(i, (i + k) % count) for i in range(count)])
                for k in range(1, count)
            ]
        )
        return jnp.sum(jnp.take(parts, (mine - jnp.arange(count)) % count, axis=0), axis=0)
    count_mp = lax.axis_size("mp")
    steps = [1 << b for b in range(count.bit_length() - 1)]
    for level in range(len(steps)):
        pairs = []
        for i in range(count):
            for m in range(count_mp):
                step = steps[level] if m % 2 == 0 else steps[len(steps) - 1 - level]
                pairs.append((i * count_mp + m, (i ^ step) * count_mp + m))
        x = x + lax.ppermute(x, ("section", "mp"), pairs)
    return x


def pad_cols(count):
    return -(-count // 128) * 128


def on_device(
    target_hidden,
    embeds,
    token_ids,
    lengths,
    offsets,
    target_gain,
    draft_gain,
    head,
    fc_embed,
    fc_feature,
):
    count_dp = lax.axis_size("dp")
    count_mp = lax.axis_size("mp")
    count_sec = lax.axis_size("section")
    groups = count_mp * count_dp
    n_dev = count_sec * groups
    my_dp = lax.axis_index("dp")
    my_mp = lax.axis_index("mp")
    my_sec = lax.axis_index("section")
    me = (my_sec * count_mp + my_mp) * count_dp + my_dp
    width = target_hidden.shape[2]
    seq_len = target_hidden.shape[1]
    vocab_tile = head.shape[0]
    block = fc_embed.shape[1]
    full_width = width * count_sec
    total_rows = R_OWN * groups
    per_dev = total_rows // n_dev
    half = 2 * R_OWN
    count_seq = lengths.shape[0]
    earlier = jnp.arange(count_seq)[None, :] < jnp.arange(count_seq)[:, None]
    starts = jnp.sum(jnp.where(earlier, lengths[None, :], 0), axis=1)

    first = jnp.minimum(offsets[my_dp] + my_mp * half, seq_len - half)
    mine = jnp.stack(
        [
            lax.dynamic_slice_in_dim(embeds[0], first, half, axis=0),
            lax.dynamic_slice_in_dim(target_hidden[0], first, half, axis=0),
        ]
    )
    every = shifted(shifted(mine, "dp"), "mp")
    every = every.transpose(2, 0, 1, 3, 4).reshape(2, count_mp * count_dp * half, width)
    packed = jnp.arange(total_rows, dtype=jnp.int32)
    seq_all, slot_all, offset_all = locate(packed, starts, lengths, offsets)
    shift_mp = (my_mp - slot_all // half) % count_mp
    shift_dp = (my_dp - seq_all) % count_dp
    base = offset_all + (slot_all // half) * half
    lag = base - jnp.minimum(base, seq_len - half)
    within = jnp.minimum(slot_all % half + lag, half - 1)
    pick = (shift_mp * count_dp + shift_dp) * half + within
    embed_all = jnp.take(every[0], pick, axis=0)
    feature_all = jnp.take(every[1], pick, axis=0)
    flat = seq_all * seq_len + offset_all + slot_all
    ids = token_ids.reshape(-1)
    labels_all = jnp.sum(
        jnp.where(jnp.arange(ids.shape[0], dtype=jnp.int32)[None, :] == flat[:, None], ids, 0),
        axis=1,
    )

    partial_value = jnp.dot(embed_all, fc_embed, preferred_element_type=jnp.float32) + jnp.dot(
        feature_all, fc_feature, preferred_element_type=jnp.float32
    )
    target_square = section_sum(jnp.sum(jnp.square(feature_all.astype(jnp.float32)), axis=1))
    target_scale = lax.rsqrt(target_square / D + eps_norm)
    target_norm = (feature_all.astype(jnp.float32) * target_scale[:, None] * target_gain).astype(
        jnp.bfloat16
    )
    target_logit = section_sum(contract_last(target_norm, head))
    piece = width // groups
    spare = pad_cols(-(-piece // per_dev))
    gain_piece = lax.dynamic_slice_in_dim(draft_gain, (my_mp * count_dp + my_dp) * piece, piece)
    extra = jnp.pad(gain_piece, (0, per_dev * spare - piece)).reshape(per_dev, spare)
    send1 = jnp.concatenate(
        [
            partial_value.reshape(n_dev, per_dev, block),
            jnp.broadcast_to(extra[None], (n_dev,) + extra.shape),
        ],
        axis=2,
    )
    got1 = exchange(send1, ALL).reshape(count_sec, groups, per_dev, -1)
    hidden = (
        jnp.sum(got1[..., :block], axis=0).transpose(1, 0, 2).reshape(per_dev, groups * block)
    )
    extra_got = got1[..., block:].reshape(count_sec, groups, per_dev * spare)
    gain_full = extra_got[:, :, :piece].reshape(full_width)
    draft_square = jnp.sum(hidden * hidden, axis=1)
    draft_scale = lax.rsqrt(draft_square / D + eps_norm)
    draft_norm = (hidden * draft_scale[:, None] * gain_full).astype(jnp.bfloat16)

    send2 = jnp.broadcast_to(
        draft_norm.reshape(per_dev, count_sec, 1, width).transpose(1, 2, 0, 3),
        (count_sec, count_dp, per_dev, width),
    ).reshape(count_sec * count_dp, per_dev, width)
    by_mp = shifted(exchange(send2, ("section", "dp")), "mp")
    by_mp = jnp.take(by_mp, (my_mp - jnp.arange(count_mp, dtype=jnp.int32)) % count_mp, axis=0)
    draft_norm_all = (
        by_mp.reshape(count_mp, count_sec, count_dp, per_dev, width)
        .transpose(1, 0, 2, 3, 4)
        .reshape(total_rows, width)
    )

    draft_logit = section_sum(contract_last(draft_norm_all, head))
    column_zero = (my_mp * count_dp + my_dp) * vocab_tile
    is_label = (
        labels_all[:, None] - column_zero == jnp.arange(vocab_tile, dtype=jnp.int32)[None, :]
    )
    target_exp = jnp.exp(target_logit)
    sums = jnp.stack(
        [
            jnp.sum(target_exp, axis=1),
            jnp.sum(target_exp * draft_logit, axis=1),
            jnp.sum(jnp.exp(draft_logit), axis=1),
            jnp.sum(jnp.where(is_label, draft_logit, 0.0), axis=1),
        ]
    )
    sums = jnp.sum(
        exchange(jnp.broadcast_to(sums[None], (groups,) + sums.shape), ("mp", "dp")), axis=0
    )
    target_total, cross_total, draft_total, label_logit = sums[0], sums[1], sums[2], sums[3]
    draft_lse = jnp.log(draft_total)
    target_lse = jnp.log(target_total)
    row_loss = (
        draft_lse
        - (1.0 - label_mix) * cross_total / target_total
        - label_mix * label_logit
        + z_weight * draft_lse * draft_lse
    )
    loss = jnp.mean(row_loss)
    grad_tile = (
        (
            (1.0 + 2.0 * z_weight * draft_lse)[:, None] * jnp.exp(draft_logit - draft_lse[:, None])
            - (1.0 - label_mix) * jnp.exp(target_logit - target_lse[:, None])
            - label_mix * is_label.astype(jnp.float32)
        )
    ).astype(jnp.bfloat16)

    grad_part = jnp.dot(grad_tile, head, preferred_element_type=jnp.float32)
    by_mp = grad_part.reshape(count_sec, count_mp, count_dp, per_dev, width).transpose(1, 0, 2, 3, 4)
    reduced = lax.dynamic_index_in_dim(by_mp, my_mp, 0, keepdims=False)
    for k in range(1, count_mp):
        reduced = reduced + lax.ppermute(
            lax.dynamic_index_in_dim(by_mp, (my_mp + k) % count_mp, 0, keepdims=False),
            "mp",
            [(i, (i + k) % count_mp) for i in range(count_mp)],
        )
    send5 = reduced.reshape(count_sec * count_dp, per_dev, width)
    got5 = exchange(send5, ("section", "dp")).reshape(count_sec, count_dp, per_dev, width)
    draft_grad = jnp.sum(got5, axis=1).transpose(1, 0, 2).reshape(per_dev, full_width)
    upstream = draft_grad * gain_full
    inner_sum = jnp.sum(hidden * upstream, axis=1)
    hidden_grad = (
        draft_scale[:, None] * upstream - hidden * (draft_scale**3 * inner_sum / D)[:, None]
    ).astype(jnp.bfloat16)

    send6 = jnp.broadcast_to(
        hidden_grad.reshape(per_dev, 1, groups, block).transpose(1, 2, 0, 3),
        (count_sec, groups, per_dev, block),
    ).reshape(n_dev, per_dev, block)
    block_grad = exchange(send6, ALL).reshape(total_rows, block)
    grad_embed = contract_first(embed_all, block_grad)
    grad_feature = contract_first(feature_all, block_grad)
    return (loss, grad_embed, grad_feature)


def solution(mesh):
    return jax.shard_map(
        on_device,
        mesh=mesh,
        in_specs=(
            P("dp", None, "section"),
            P("dp", None, "section"),
            P(),
            P(),
            P(),
            P("section"),
            P("section"),
            P(("mp", "dp"), "section"),
            P("section", ("mp", "dp")),
            P("section", ("mp", "dp")),
        ),
        out_specs=(P(), P("section", ("mp", "dp")), P("section", ("mp", "dp"))),
        check_vma=False,
    )
```

```python
import jax
import jax.numpy as jnp
from jax import lax
from jax.sharding import PartitionSpec as P

D = 8192
R_OWN = 8


z_weight = 0.004
label_mix = 0.1
eps_norm = 1e-05

ALL = ("section", "mp", "dp")


def contract_last(operand, weights):
    return lax.dot_general(
        operand, weights, (((1,), (1,)), ((), ())), preferred_element_type=jnp.float32
    )


def contract_first(operand, weights):
    return lax.dot_general(
        operand, weights, (((0,), (0,)), ((), ())), preferred_element_type=jnp.float32
    )


def locate(packed, starts, lengths, offsets):
    rel = packed[:, None] - starts[None, :]
    inside = (rel >= 0) & (rel < lengths[None, :])
    seq = jnp.sum(jnp.where(inside, jnp.arange(starts.shape[0], dtype=jnp.int32)[None, :], 0), axis=1)
    slot = jnp.sum(jnp.where(inside, rel, 0), axis=1)
    offset = jnp.sum(jnp.where(inside, offsets[None, :], 0), axis=1)
    return seq, slot, offset


def exchange(send, axes):
    return lax.all_to_all(send, axes, split_axis=0, concat_axis=0, tiled=True)


def shifted(x, axis):
    count = lax.axis_size(axis)
    parts = [x] + [
        lax.ppermute(x, axis, [(i, (i + k) % count) for i in range(count)])
        for k in range(1, count)
    ]
    return jnp.stack(parts)


def section_sum(x):
    count = lax.axis_size("section")
    if count & (count - 1):
        mine = lax.axis_index("section")
        parts = jnp.stack(
            [x]
            + [
                lax.ppermute(x, "section", [(i, (i + k) % count) for i in range(count)])
                for k in range(1, count)
            ]
        )
        return jnp.sum(jnp.take(parts, (mine - jnp.arange(count)) % count, axis=0), axis=0)
    count_mp = lax.axis_size("mp")
    steps = [1 << b for b in range(count.bit_length() - 1)]
    for level in range(len(steps)):
        pairs = []
        for i in range(count):
            for m in range(count_mp):
                step = steps[level] if m % 2 == 0 else steps[len(steps) - 1 - level]
                pairs.append((i * count_mp + m, (i ^ step) * count_mp + m))
        x = x + lax.ppermute(x, ("section", "mp"), pairs)
    return x


def pad_cols(count):
    return -(-count // 128) * 128


def on_device(
    target_hidden,
    embeds,
    token_ids,
    lengths,
    offsets,
    target_gain,
    draft_gain,
    head,
    fc_embed,
    fc_feature,
):
    count_dp = lax.axis_size("dp")
    count_mp = lax.axis_size("mp")
    count_sec = lax.axis_size("section")
    groups = count_mp * count_dp
    n_dev = count_sec * groups
    my_dp = lax.axis_index("dp")
    my_mp = lax.axis_index("mp")
    my_sec = lax.axis_index("section")
    me = (my_sec * count_mp + my_mp) * count_dp + my_dp
    width = target_hidden.shape[2]
    seq_len = target_hidden.shape[1]
    vocab_tile = head.shape[0]
    block = fc_embed.shape[1]
    full_width = width * count_sec
    total_rows = R_OWN * groups
    per_dev = total_rows // n_dev
    half = 2 * R_OWN
    count_seq = lengths.shape[0]
    earlier = jnp.arange(count_seq)[None, :] < jnp.arange(count_seq)[:, None]
    starts = jnp.sum(jnp.where(earlier, lengths[None, :], 0), axis=1)

    first = jnp.minimum(offsets[my_dp] + my_mp * half, seq_len - half)
    mine = jnp.stack(
        [
            lax.dynamic_slice_in_dim(embeds[0], first, half, axis=0),
            lax.dynamic_slice_in_dim(target_hidden[0], first, half, axis=0),
        ]
    )
    every = shifted(shifted(mine, "dp"), "mp")
    every = every.transpose(2, 0, 1, 3, 4).reshape(2, count_mp * count_dp * half, width)
    packed = jnp.arange(total_rows, dtype=jnp.int32)
    seq_all, slot_all, offset_all = locate(packed, starts, lengths, offsets)
    shift_mp = (my_mp - slot_all // half) % count_mp
    shift_dp = (my_dp - seq_all) % count_dp
    base = offset_all + (slot_all // half) * half
    lag = base - jnp.minimum(base, seq_len - half)
    within = jnp.minimum(slot_all % half + lag, half - 1)
    pick = (shift_mp * count_dp + shift_dp) * half + within
    embed_all = jnp.take(every[0], pick, axis=0)
    feature_all = jnp.take(every[1], pick, axis=0)
    flat = seq_all * seq_len + offset_all + slot_all
    ids = token_ids.reshape(-1)
    labels_all = jnp.sum(
        jnp.where(jnp.arange(ids.shape[0], dtype=jnp.int32)[None, :] == flat[:, None], ids, 0),
        axis=1,
    )

    partial_value = jnp.dot(embed_all, fc_embed, preferred_element_type=jnp.float32) + jnp.dot(
        feature_all, fc_feature, preferred_element_type=jnp.float32
    )
    target_square = jnp.sum(jnp.square(feature_all.astype(jnp.float32)), axis=1)
    piece = width // groups
    spare = pad_cols(-(-(total_rows + piece) // per_dev))
    gain_piece = lax.dynamic_slice_in_dim(draft_gain, (my_mp * count_dp + my_dp) * piece, piece)
    extra = jnp.pad(
        jnp.concatenate([target_square, gain_piece]),
        (0, per_dev * spare - total_rows - piece),
    ).reshape(per_dev, spare)
    send1 = jnp.concatenate(
        [
            partial_value.reshape(n_dev, per_dev, block),
            jnp.broadcast_to(extra[None], (n_dev,) + extra.shape),
        ],
        axis=2,
    )
    got1 = exchange(send1, ALL).reshape(count_sec, groups, per_dev, -1)
    hidden = (
        jnp.sum(got1[..., :block], axis=0).transpose(1, 0, 2).reshape(per_dev, groups * block)
    )
    extra_got = got1[..., block:].reshape(count_sec, groups, per_dev * spare)
    target_square = jnp.sum(extra_got[:, 0, :total_rows], axis=0)
    gain_full = extra_got[:, :, total_rows : total_rows + piece].reshape(full_width)
    target_scale = lax.rsqrt(target_square / D + eps_norm)
    target_norm = (feature_all.astype(jnp.float32) * target_scale[:, None] * target_gain).astype(
        jnp.bfloat16
    )
    target_logit = section_sum(contract_last(target_norm, head))
    draft_square = jnp.sum(hidden * hidden, axis=1)
    draft_scale = lax.rsqrt(draft_square / D + eps_norm)
    draft_norm = (hidden * draft_scale[:, None] * gain_full).astype(jnp.bfloat16)

    send2 = jnp.broadcast_to(
        draft_norm.reshape(per_dev, count_sec, 1, width).transpose(1, 2, 0, 3),
        (count_sec, groups, per_dev, width),
    ).reshape(n_dev, per_dev, width)
    draft_norm_all = exchange(send2, ALL).reshape(total_rows, width)

    draft_logit = section_sum(contract_last(draft_norm_all, head))
    column_zero = (my_mp * count_dp + my_dp) * vocab_tile
    is_label = (
        labels_all[:, None] - column_zero == jnp.arange(vocab_tile, dtype=jnp.int32)[None, :]
    )
    target_exp = jnp.exp(target_logit)
    sums = jnp.stack(
        [
            jnp.sum(target_exp, axis=1),
            jnp.sum(target_exp * draft_logit, axis=1),
            jnp.sum(jnp.exp(draft_logit), axis=1),
            jnp.sum(jnp.where(is_label, draft_logit, 0.0), axis=1),
        ]
    )
    sums = jnp.sum(
        exchange(jnp.broadcast_to(sums[None], (groups,) + sums.shape), ("mp", "dp")), axis=0
    )
    target_total, cross_total, draft_total, label_logit = sums[0], sums[1], sums[2], sums[3]
    draft_lse = jnp.log(draft_total)
    target_lse = jnp.log(target_total)
    row_loss = (
        draft_lse
        - (1.0 - label_mix) * cross_total / target_total
        - label_mix * label_logit
        + z_weight * draft_lse * draft_lse
    )
    loss = jnp.mean(row_loss)
    grad_tile = (
        (
            (1.0 + 2.0 * z_weight * draft_lse)[:, None] * jnp.exp(draft_logit - draft_lse[:, None])
            - (1.0 - label_mix) * jnp.exp(target_logit - target_lse[:, None])
            - label_mix * is_label.astype(jnp.float32)
        )
    ).astype(jnp.bfloat16)

    grad_part = jnp.dot(grad_tile, head, preferred_element_type=jnp.float32)
    by_mp = grad_part.reshape(count_sec, count_mp, count_dp, per_dev, width).transpose(1, 0, 2, 3, 4)
    reduced = lax.dynamic_index_in_dim(by_mp, my_mp, 0, keepdims=False)
    for k in range(1, count_mp):
        reduced = reduced + lax.ppermute(
            lax.dynamic_index_in_dim(by_mp, (my_mp + k) % count_mp, 0, keepdims=False),
            "mp",
            [(i, (i + k) % count_mp) for i in range(count_mp)],
        )
    send5 = reduced.reshape(count_sec * count_dp, per_dev, width)
    got5 = exchange(send5, ("section", "dp")).reshape(count_sec, count_dp, per_dev, width)
    draft_grad = jnp.sum(got5, axis=1).transpose(1, 0, 2).reshape(per_dev, full_width)
    upstream = draft_grad * gain_full
    inner_sum = jnp.sum(hidden * upstream, axis=1)
    hidden_grad = (
        draft_scale[:, None] * upstream - hidden * (draft_scale**3 * inner_sum / D)[:, None]
    ).astype(jnp.bfloat16)

    send6 = jnp.broadcast_to(
        hidden_grad.reshape(per_dev, 1, groups, block).transpose(1, 2, 0, 3),
        (count_sec, groups, per_dev, block),
    ).reshape(n_dev, per_dev, block)
    block_grad = exchange(send6, ALL).reshape(total_rows, block)
    grad_embed = contract_first(embed_all, block_grad)
    grad_feature = contract_first(feature_all, block_grad)
    return (loss, grad_embed, grad_feature)


def solution(mesh):
    return jax.shard_map(
        on_device,
        mesh=mesh,
        in_specs=(
            P("dp", None, "section"),
            P("dp", None, "section"),
            P(),
            P(),
            P(),
            P("section"),
            P("section"),
            P(("mp", "dp"), "section"),
            P("section", ("mp", "dp")),
            P("section", ("mp", "dp")),
        ),
        out_specs=(P(), P("section", ("mp", "dp")), P("section", ("mp", "dp"))),
        check_vma=False,
    )
```
